32 devices in a mesh: vis: 16 (over z, y, x), chan: 2 (over core).
Axes of the slice: x: 2, y: 2, z: 4, core: 2. Of those that a mesh axis runs over, the one named last changes fastest.
Arguments:
- patch_intensity: float32 [512, 2, 2, 512], P('vis', 'chan'), may hold values from -6 to 6
- recorded_samples: float32 [2, 2, 16384], P('chan', None, 'vis'), may hold values from -6 to 6
- sample_importance: float32 [16384], P('vis'), may hold values from 0.3 to 3
- block_populations: int32 [64], P('vis'), may hold values from 64 to 256, as said below
- receiver_pairs: int32 [16384, 2], P('vis'), may hold values from 0 to 511
- sample_rotation_phase: float32 [16384], P('vis'), may hold values from -1 to 1
- spectral_scaling: float32 [2], P('chan'), may hold values from 0.7 to 1.4
- receiver_positions: float32 [2, 512], replicated, may hold values from -2500 to 2500
- patch_layout_position: int32 [2, 2], replicated, may hold values from 0 to 63
Outputs:
- new_sky: float32 [512, 2, 2, 512], P('vis', 'chan')
- residual: float32 [2, 2, 16384], P('chan', None, 'vis')
The draws below stay inside these ranges and needn't reach their ends.
Inputs may be any that keep to these rules, and one draw needn't show every extreme that they name: `block_populations`: live visibility slots of each block; some block is full.
All inputs are finite; a program needn't handle non-finite values.
Results may differ from the reference program's by a relative error of at most 0.006.
Values may be sent and summed in bfloat16 or wider, within the bound.
No kernel may reach another device: no remote copies, remote signals or barrier semaphores. Data moves between devices by JAX's collectives and lax.ppermute only.
A program may use at most 128 MiB of HBM per device.

```python
import math
import jax
import jax.numpy as jnp
from jax import lax

FACET = 512
GRID = 64
FACETS = 2
RECEIVER_TOTAL = 512
BLOCK = 256
NV_DEV = 1024
SAMPLE_PLACES = 16384
BLOCKS = 64
CHANNELS = 2
N_VIS = 16


def draw_block_populations(key, part):
    drawn_counts = jax.random.randint(key, (BLOCKS,), BLOCK // 4, BLOCK + 1)
    chosen_block = jax.random.randint(jax.random.fold_in(key, 7), (), 0, BLOCKS)
    return jnp.where(jnp.arange(BLOCKS) == chosen_block, BLOCK, drawn_counts).astype(jnp.int32)


def plant(drawn, rng, least, top_value):
    dims = drawn.shape
    place = [jax.random.randint(jax.random.fold_in(rng, axis), (), 0, dims[axis]) for axis in range(len(dims))]
    drawn = drawn.at[tuple(place)].set(least)
    longest = dims.index(max(dims))
    place[longest] = (place[longest] + 1) % dims[longest]
    return drawn.at[tuple(place)].set(top_value)


def level_of(rng, extent, shards, low, high):
    level = 1.0
    for axis_at, shards_of in shards:
        draws = jax.random.uniform(jax.random.fold_in(jax.random.fold_in(rng, 6), axis_at), (shards_of,), jnp.float32, low / len(shards), high / len(shards))
        level = level * jnp.repeat(jnp.exp(draws), extent[axis_at] // shards_of).reshape((-1,) + (1,) * (len(extent) - 1 - axis_at))
    return level


def scatter_about(rng, dims, deviation, bound, cuts=(), kind=jnp.bfloat16):
    level = level_of(rng, dims, cuts, -0.22, 0.18) if cuts else 1.0
    array = jax.random.normal(rng, dims, jnp.float32) * deviation * level
    return jnp.minimum(jnp.maximum(array, -bound), bound).astype(kind)


def setup_inputs(seed: int = 0) -> dict:
    streams_of = jax.random.split(jax.random.key(seed), 10)
    patch_intensity = scatter_about(streams_of[0], (FACET, CHANNELS, FACETS, FACET), 1.0, 6.0, ((0, 16), (1, 2)), jnp.float32)
    recorded_samples = scatter_about(streams_of[1], (CHANNELS, 2, SAMPLE_PLACES), 1.0, 6.0, ((0, 2), (2, 16)), jnp.float32)
    sample_importance = jnp.clip(jnp.exp(math.log(3.0) - 2.3025851 * jax.random.uniform(streams_of[2], (SAMPLE_PLACES,), jnp.float32) ** level_of(streams_of[2], (SAMPLE_PLACES,), ((0, 16),), -0.2, 0.2)), 0.3, 3.0)
    block_populations = draw_block_populations(jax.random.fold_in(streams_of[9], 71), 0)
    receiver_pairs = plant(jax.random.randint(streams_of[4], (SAMPLE_PLACES, 2), 0, RECEIVER_TOTAL), jax.random.fold_in(streams_of[4], 1), 0, RECEIVER_TOTAL - 1).astype(jnp.int32)
    sample_rotation_phase = jnp.clip(jax.random.uniform(streams_of[5], (SAMPLE_PLACES,), jnp.float32, -1.0, 1.0) * level_of(streams_of[5], (SAMPLE_PLACES,), ((0, 16),), -0.4, 0.0), -1.0, 1.0)
    spectral_scaling = jnp.clip(jnp.exp(math.log(1.4) - 0.6931472 * jax.random.uniform(streams_of[6], (CHANNELS,), jnp.float32) ** level_of(streams_of[6], (CHANNELS,), ((0, 2),), -0.2, 0.2)), 0.7, 1.4)
    receiver_positions = jnp.clip(jax.random.uniform(streams_of[7], (2, RECEIVER_TOTAL), jnp.float32, -2500.0, 2500.0), -2500.0, 2500.0)
    patch_layout_position = plant(jax.random.randint(streams_of[8], (FACETS, 2), 0, GRID), jax.random.fold_in(streams_of[8], 1), 0, GRID - 1).astype(jnp.int32)
    return {"patch_intensity": patch_intensity, "recorded_samples": recorded_samples, "sample_importance": sample_importance, "block_populations": block_populations, "receiver_pairs": receiver_pairs, "sample_rotation_phase": sample_rotation_phase, "spectral_scaling": spectral_scaling, "receiver_positions": receiver_positions, "patch_layout_position": patch_layout_position}


full_turn = 6.283185307179586
step_size = 0.5
smooth_weight = 0.5

def pixel_pos(grid_index, offsets, facet, image):
    return (grid_index * facet + offsets - image // 2).astype(jnp.float32) / float(image)

def row_tables(coord, grid_rows, start, count, facet, image):
    places = pixel_pos(grid_rows[:, None], start + jnp.arange(count, dtype=jnp.int32)[None, :], facet, image)
    theta = coord[:, None, :, None] * places[None, :, None, :]
    return (jnp.cos(full_turn * theta), jnp.sin(full_turn * theta))

def col_tables(coord, grid_cols, facet, image):
    places = pixel_pos(grid_cols[:, None], jnp.arange(facet, dtype=jnp.int32)[None, :], facet, image)
    theta = coord[:, None, :, None] * places[None, :, None, :]
    return (jnp.cos(full_turn * theta).astype(jnp.bfloat16), jnp.sin(full_turn * theta).astype(jnp.bfloat16))

def reference(patch_intensity, recorded_samples, sample_importance, block_populations, receiver_pairs, sample_rotation_phase, spectral_scaling, receiver_positions, patch_layout_position):
    image = GRID * FACET
    leading_receiver = receiver_positions[:, receiver_pairs[:, 0]]
    trailing_receiver = receiver_positions[:, receiver_pairs[:, 1]]
    eastward_shift = leading_receiver[0] - trailing_receiver[0]
    northward_shift = leading_receiver[1] - trailing_receiver[1]
    base_u = eastward_shift * jnp.cos(sample_rotation_phase) - northward_shift * jnp.sin(sample_rotation_phase)
    base_v = eastward_shift * jnp.sin(sample_rotation_phase) + northward_shift * jnp.cos(sample_rotation_phase)
    slots = jnp.arange(SAMPLE_PLACES, dtype=jnp.int32)
    live = (slots % BLOCK < block_populations[slots // BLOCK]).astype(jnp.float32)
    scale_vis = live * sample_importance
    sky_half = patch_intensity.astype(jnp.bfloat16)
    norm_pred = 1.0 / math.sqrt(FACETS * FACET * FACET)
    norm_grad = 1.0 / math.sqrt(SAMPLE_PLACES)

    def one_channel(index):
        freq = spectral_scaling[index]
        coord_u = (freq * base_u).reshape(N_VIS, NV_DEV)
        coord_v = (freq * base_v).reshape(N_VIS, NV_DEV)
        obs_re = recorded_samples[index, 0].reshape(N_VIS, NV_DEV)
        obs_im = recorded_samples[index, 1].reshape(N_VIS, NV_DEV)
        scales = scale_vis.reshape(N_VIS, NV_DEV)
        sky_one = lax.dynamic_slice_in_dim(sky_half, index, 1, 1).astype(jnp.float32)

        def block_step(total, inputs):
            part_u, part_v, part_re, part_im, part_scale = inputs
            row_cos, row_sin = row_tables(part_u[None], patch_layout_position[:, 0], 0, FACET, FACET, image)
            col_cos, col_sin = col_tables(part_v[None], patch_layout_position[:, 1], FACET, image)
            col_cos = col_cos.astype(jnp.float32)
            col_sin = col_sin.astype(jnp.float32)
            wave_c = jnp.einsum('cfkj,icfj->cfki', col_cos, sky_one)
            wave_s = jnp.einsum('cfkj,icfj->cfki', col_sin, sky_one)
            pred_re = norm_pred * lax.optimization_barrier(jnp.sum(row_cos * wave_c - row_sin * wave_s, axis=(1, 3)))[0]
            pred_im = -norm_pred * lax.optimization_barrier(jnp.sum(row_cos * wave_s + row_sin * wave_c, axis=(1, 3)))[0]
            resid_real = part_scale * (pred_re - part_re)
            resid_imag = part_scale * (pred_im - part_im)
            z_one = (row_cos * resid_real[None, None, :, None] - row_sin * resid_imag[None, None, :, None]).astype(jnp.bfloat16)
            z_two = (row_sin * resid_real[None, None, :, None] + row_cos * resid_imag[None, None, :, None]).astype(jnp.bfloat16)
            total = total + jnp.einsum('cfki,cfkj->icfj', z_one.astype(jnp.float32), col_cos)
            total = total - jnp.einsum('cfki,cfkj->icfj', z_two.astype(jnp.float32), col_sin)
            return (total, jnp.stack([resid_real, resid_imag], axis=0))
        start = jnp.zeros((FACET, 1, FACETS, FACET), jnp.float32)
        total, resid = lax.scan(block_step, start, (coord_u, coord_v, obs_re, obs_im, scales))
        return (total[:, 0], jnp.transpose(resid, (1, 0, 2)).reshape(2, SAMPLE_PLACES))
    grads, residual = lax.map(one_channel, jnp.arange(CHANNELS, dtype=jnp.int32))
    gradient = norm_grad * jnp.transpose(grads, (1, 0, 2, 3))
    diffs = patch_intensity[:, 1:] - patch_intensity[:, :-1]
    smooth = jnp.pad(diffs, ((0, 0), (1, 0), (0, 0), (0, 0))) - jnp.pad(diffs, ((0, 0), (0, 1), (0, 0), (0, 0)))
    new_sky = patch_intensity - step_size * (gradient + smooth_weight * smooth)
    return (new_sky, residual)
```

```python
import math

import jax
import jax.numpy as jnp
from jax import lax
from jax.sharding import PartitionSpec as P

GRID = 64
BLOCK = 256


full_turn = 6.283185307179586
step_size = 0.5
smooth_weight = 0.5


def extended(cells, sides, width):
    for axis, dim in sides:
        count = lax.axis_size(axis)
        ends = count - 1
        head = lax.slice_in_dim(cells, 0, width, axis=dim)
        tail = lax.slice_in_dim(cells, cells.shape[dim] - width, cells.shape[dim], axis=dim)
        cells = jnp.concatenate(
            [
                lax.ppermute(tail, axis, [(i, (i + 1) % count) for i in range(ends)]),
                cells,
                lax.ppermute(head, axis, [((i + 1) % count, i) for i in range(ends)]),
            ],
            axis=dim,
        )
    return cells


def pixel_pos(grid_index, offsets, facet, image):
    return (grid_index * facet + offsets - image // 2).astype(jnp.float32) / float(image)


def row_tables(coord, grid_rows, count, facet, image):
    places = pixel_pos(
        grid_rows[:, None], jnp.arange(count, dtype=jnp.int32)[None, :], facet, image
    )
    theta = coord[:, None, :, None] * places[None, :, None, :]
    return (jnp.cos(full_turn * theta), jnp.sin(full_turn * theta))


def col_tables(coord, grid_cols, facet, image):
    places = pixel_pos(
        grid_cols[:, None], jnp.arange(facet, dtype=jnp.int32)[None, :], facet, image
    )
    theta = coord[:, None, :, None] * places[None, :, None, :]
    return (
        jnp.cos(full_turn * theta).astype(jnp.bfloat16),
        jnp.sin(full_turn * theta).astype(jnp.bfloat16),
    )


def receiver_lookup_dict(table_row, antenna_ids):
    numbers = jnp.arange(table_row.shape[0], dtype=jnp.int32)
    return jnp.sum(
        jnp.where(antenna_ids[:, None] == numbers[None, :], table_row[None, :], 0.0), axis=1
    )


def predict_terms(row_cos, row_sin, col_cos, col_sin, sky_rows):
    wave_c = jnp.einsum("cfkj,icfj->cfki", col_cos, sky_rows, preferred_element_type=jnp.float32)
    wave_s = jnp.einsum("cfkj,icfj->cfki", col_sin, sky_rows, preferred_element_type=jnp.float32)
    sum_re = jnp.sum(row_cos * wave_c - row_sin * wave_s, axis=(1, 3))
    sum_im = -jnp.sum(row_cos * wave_s + row_sin * wave_c, axis=(1, 3))
    return (sum_re, sum_im)


def back_terms(row_cos, row_sin, col_cos, col_sin, resid_real, resid_imag):
    real_b = resid_real[:, None, :, None]
    imag_b = resid_imag[:, None, :, None]
    z_one = (row_cos * real_b - row_sin * imag_b).astype(jnp.bfloat16)
    z_two = (row_sin * real_b + row_cos * imag_b).astype(jnp.bfloat16)
    first_term = jnp.einsum("cfki,cfkj->icfj", z_one, col_cos, preferred_element_type=jnp.float32)
    return first_term - jnp.einsum(
        "cfki,cfkj->icfj", z_two, col_sin, preferred_element_type=jnp.float32
    )


def local(
    patch_intensity,
    recorded_samples,
    sample_importance,
    block_populations,
    receiver_pairs,
    sample_rotation_phase,
    spectral_scaling,
    receiver_positions,
    patch_layout_position,
):
    rows_dev = patch_intensity.shape[0]
    ch_local = patch_intensity.shape[1]
    facets_here = patch_intensity.shape[2]
    facet = patch_intensity.shape[3]
    nvis = sample_importance.shape[0]
    image = GRID * facet
    norm_pred = 1.0 / math.sqrt(facets_here * facet * facet)
    norm_grad = 1.0 / math.sqrt(nvis * lax.axis_size("vis"))
    eastward_shift = receiver_lookup_dict(
        receiver_positions[0], receiver_pairs[:, 0]
    ) - receiver_lookup_dict(receiver_positions[0], receiver_pairs[:, 1])
    northward_shift = receiver_lookup_dict(
        receiver_positions[1], receiver_pairs[:, 0]
    ) - receiver_lookup_dict(receiver_positions[1], receiver_pairs[:, 1])
    base_u = eastward_shift * jnp.cos(sample_rotation_phase) - northward_shift * jnp.sin(
        sample_rotation_phase
    )
    base_v = eastward_shift * jnp.sin(sample_rotation_phase) + northward_shift * jnp.cos(
        sample_rotation_phase
    )
    coord_u = spectral_scaling[:, None] * base_u[None, :]
    coord_v = spectral_scaling[:, None] * base_v[None, :]
    slots = jnp.arange(nvis, dtype=jnp.int32)
    block_of = slots // BLOCK
    block_numbers = jnp.arange(block_populations.shape[0], dtype=jnp.int32)
    block_count = jnp.sum(
        jnp.where(block_of[:, None] == block_numbers[None, :], block_populations[None, :], 0),
        axis=1,
    )
    scale_vis = (slots % BLOCK < block_count).astype(jnp.float32) * sample_importance
    sky_half = patch_intensity.astype(jnp.bfloat16)
    grid_rows = patch_layout_position[:, 0]
    grid_cols = patch_layout_position[:, 1]
    col_cos, col_sin = col_tables(coord_v, grid_cols, facet, image)
    n_vis = lax.axis_size("vis")
    piece = lax.all_to_all(
        jnp.broadcast_to(sky_half[None], (n_vis,) + sky_half.shape).reshape(
            (n_vis * rows_dev,) + sky_half.shape[1:]
        ),
        "vis",
        0,
        0,
        tiled=True,
    )
    row_cos, row_sin = row_tables(coord_u, grid_rows, piece.shape[0], facet, image)
    sum_re, sum_im = predict_terms(row_cos, row_sin, col_cos, col_sin, piece)
    resid_real = scale_vis[None, :] * (norm_pred * sum_re - recorded_samples[:, 0])
    resid_imag = scale_vis[None, :] * (norm_pred * sum_im - recorded_samples[:, 1])
    row_cos, row_sin = row_tables(coord_u, grid_rows, lax.axis_size("vis") * rows_dev, facet, image)
    parts = lax.all_to_all(
        back_terms(row_cos, row_sin, col_cos, col_sin, resid_real, resid_imag),
        "vis",
        0,
        0,
        tiled=True,
    )
    gradient = jnp.sum(parts.reshape((n_vis, rows_dev) + parts.shape[1:]), axis=0)
    padded = extended(patch_intensity.astype(jnp.bfloat16), (("chan", 1),), 1).astype(
        patch_intensity.dtype
    )
    left_side = padded[:, :-2]
    right_side = padded[:, 2:]
    chan_index = lax.axis_index("chan") * ch_local + jnp.arange(ch_local, dtype=jnp.int32)
    total_chan = ch_local * lax.axis_size("chan")
    has_left = (chan_index >= 1).astype(jnp.float32)[None, :, None, None]
    has_right = (chan_index <= total_chan - 2).astype(jnp.float32)[None, :, None, None]
    smooth = has_left * (patch_intensity - left_side) + has_right * (patch_intensity - right_side)
    new_sky = patch_intensity - step_size * (norm_grad * gradient + smooth_weight * smooth)
    residual = jnp.stack([resid_real, resid_imag], axis=1)
    return (new_sky, residual)


def solution(mesh):
    return jax.shard_map(
        local,
        mesh=mesh,
        in_specs=(
            P("vis", "chan", None, None),
            P("chan", None, "vis"),
            P("vis"),
            P("vis"),
            P("vis", None),
            P("vis"),
            P("chan"),
            P(),
            P(),
        ),
        out_specs=(P("vis", "chan", None, None), P("chan", None, "vis")),
        check_vma=False,
    )
```

```python
import math

import jax
import jax.numpy as jnp
from jax import lax
from jax.sharding import PartitionSpec as P

GRID = 64
BLOCK = 256
LANE_BLOCK = 128
COORD_STEPS = 16


full_turn = 6.283185307179586
step_size = 0.5
smooth_weight = 0.5


def extended(cells, sides, width):
    for axis, dim in sides:
        count = lax.axis_size(axis)
        ends = count - 1
        head = lax.slice_in_dim(cells, 0, width, axis=dim)
        tail = lax.slice_in_dim(cells, cells.shape[dim] - width, cells.shape[dim], axis=dim)
        cells = jnp.concatenate(
            [
                lax.ppermute(tail, axis, [(i, (i + 1) % count) for i in range(ends)]),
                cells,
                lax.ppermute(head, axis, [((i + 1) % count, i) for i in range(ends)]),
            ],
            axis=dim,
        )
    return cells


def receiver_lookup_dict(table_row, antenna_ids):
    numbers = jnp.arange(table_row.shape[0], dtype=jnp.int32)
    return jnp.sum(
        jnp.where(antenna_ids[:, None] == numbers[None, :], table_row[None, :], 0.0), axis=1
    )


def turns(coord, pixel, image):
    whole = jnp.round(coord * COORD_STEPS).astype(jnp.int32)
    rest = coord - whole.astype(jnp.float32) / COORD_STEPS
    period = COORD_STEPS * image
    exact = jnp.bitwise_and(whole[None, :] * pixel, period - 1).astype(jnp.float32) / period
    return exact + rest[None, :] * pixel.astype(jnp.float32) / image


def phase_table(coord, first_pixel, facet, image):
    blocks = facet // LANE_BLOCK
    starts = first_pixel[:, None] + LANE_BLOCK * jnp.arange(blocks, dtype=jnp.int32)[None, :]
    coarse = full_turn * turns(coord, starts.reshape(-1, 1), image)
    fine = full_turn * turns(coord, jnp.arange(LANE_BLOCK, dtype=jnp.int32)[:, None], image)
    coarse_c, coarse_s, fine_c, fine_s = lax.optimization_barrier(
        (jnp.cos(coarse), jnp.sin(coarse), jnp.cos(fine), jnp.sin(fine))
    )
    count = coord.shape[0]
    faces = first_pixel.shape[0]

    def spread(a):
        return jnp.broadcast_to(
            a.reshape(faces, blocks, 1, count), (faces, blocks, LANE_BLOCK, count)
        ).reshape(faces, facet, count)

    def tile(a):
        return jnp.broadcast_to(a[None, None], (faces, blocks, LANE_BLOCK, count)).reshape(
            faces, facet, count
        )

    pc, ps, qc, qs = spread(coarse_c), spread(coarse_s), tile(fine_c), tile(fine_s)
    return (pc * qc - ps * qs, ps * qc + pc * qs)


def local(
    patch_intensity,
    recorded_samples,
    sample_importance,
    block_populations,
    receiver_pairs,
    sample_rotation_phase,
    spectral_scaling,
    receiver_positions,
    patch_layout_position,
):
    rows_dev = patch_intensity.shape[0]
    ch_local = patch_intensity.shape[1]
    facets_here = patch_intensity.shape[2]
    facet = patch_intensity.shape[3]
    nvis = sample_importance.shape[0]
    n_vis = lax.axis_size("vis")
    image = GRID * facet
    norm_pred = 1.0 / math.sqrt(facets_here * facet * facet)
    norm_grad = 1.0 / math.sqrt(nvis * n_vis)
    eastward_shift = receiver_lookup_dict(
        receiver_positions[0], receiver_pairs[:, 0]
    ) - receiver_lookup_dict(receiver_positions[0], receiver_pairs[:, 1])
    northward_shift = receiver_lookup_dict(
        receiver_positions[1], receiver_pairs[:, 0]
    ) - receiver_lookup_dict(receiver_positions[1], receiver_pairs[:, 1])
    base_u = eastward_shift * jnp.cos(sample_rotation_phase) - northward_shift * jnp.sin(
        sample_rotation_phase
    )
    base_v = eastward_shift * jnp.sin(sample_rotation_phase) + northward_shift * jnp.cos(
        sample_rotation_phase
    )
    slots = jnp.arange(nvis, dtype=jnp.int32)
    block_of = slots // BLOCK
    block_numbers = jnp.arange(block_populations.shape[0], dtype=jnp.int32)
    block_count = jnp.sum(
        jnp.where(block_of[:, None] == block_numbers[None, :], block_populations[None, :], 0),
        axis=1,
    )
    scale_vis = (slots % BLOCK < block_count).astype(jnp.float32) * sample_importance
    sky_half = patch_intensity.astype(jnp.bfloat16)
    first_row = patch_layout_position[:, 0] * facet - image // 2
    first_col = patch_layout_position[:, 1] * facet - image // 2

    piece = lax.all_to_all(
        jnp.broadcast_to(sky_half[None], (n_vis,) + sky_half.shape).reshape(
            (n_vis * rows_dev,) + sky_half.shape[1:]
        ),
        "vis",
        0,
        0,
        tiled=True,
    )

    new_rows = []
    residuals = []
    for c in range(ch_local):
        coord_u = spectral_scaling[c] * base_u
        coord_v = spectral_scaling[c] * base_v
        row_cos, row_sin = phase_table(coord_u, first_row, facet, image)
        col_cos, col_sin = phase_table(coord_v, first_col, facet, image)
        cols = lax.optimization_barrier(
            jnp.concatenate([col_cos, col_sin], axis=2).astype(jnp.bfloat16)
        )
        sky_rows = jnp.transpose(piece[:, c], (1, 0, 2))
        waves = jnp.einsum("fij,fjk->fik", sky_rows, cols, preferred_element_type=jnp.float32)
        wave_c = waves[:, :, :nvis]
        wave_s = waves[:, :, nvis:]
        sum_re = jnp.sum(row_cos * wave_c - row_sin * wave_s, axis=(0, 1))
        sum_im = -jnp.sum(row_cos * wave_s + row_sin * wave_c, axis=(0, 1))
        resid_real = scale_vis * (norm_pred * sum_re - recorded_samples[c, 0])
        resid_imag = scale_vis * (norm_pred * sum_im - recorded_samples[c, 1])
        z_one = (row_cos * resid_real[None, None, :] - row_sin * resid_imag[None, None, :]).astype(
            jnp.bfloat16
        )
        z_two = (row_sin * resid_real[None, None, :] + row_cos * resid_imag[None, None, :]).astype(
            jnp.bfloat16
        )
        zs = jnp.concatenate([z_one, -z_two], axis=2)
        grad = jnp.einsum("fik,fjk->ifj", zs, cols, preferred_element_type=jnp.float32)
        new_rows.append(grad)
        residuals.append(jnp.stack([resid_real, resid_imag], axis=0))
    partial = jnp.stack(new_rows, axis=1)
    parts = lax.all_to_all(partial, "vis", 0, 0, tiled=True)
    gradient = jnp.sum(parts.reshape((n_vis, rows_dev) + parts.shape[1:]), axis=0)
    padded = extended(patch_intensity.astype(jnp.bfloat16), (("chan", 1),), 1).astype(
        patch_intensity.dtype
    )
    left_side = padded[:, :-2]
    right_side = padded[:, 2:]
    chan_index = lax.axis_index("chan") * ch_local + jnp.arange(ch_local, dtype=jnp.int32)
    total_chan = ch_local * lax.axis_size("chan")
    has_left = (chan_index >= 1).astype(jnp.float32)[None, :, None, None]
    has_right = (chan_index <= total_chan - 2).astype(jnp.float32)[None, :, None, None]
    smooth = has_left * (patch_intensity - left_side) + has_right * (patch_intensity - right_side)
    new_sky = patch_intensity - step_size * (norm_grad * gradient + smooth_weight * smooth)
    residual = jnp.stack(residuals, axis=0)
    return (new_sky, residual)


def solution(mesh):
    return jax.shard_map(
        local,
        mesh=mesh,
        in_specs=(
            P("vis", "chan", None, None),
            P("chan", None, "vis"),
            P("vis"),
            P("vis"),
            P("vis", None),
            P("vis"),
            P("chan"),
            P(),
            P(),
        ),
        out_specs=(P("vis", "chan", None, None), P("chan", None, "vis")),
        check_vma=False,
    )
```

```python
import math

import jax
import jax.numpy as jnp
from jax import lax
from jax.sharding import PartitionSpec as P

GRID = 64
BLOCK = 256
LANE_BLOCK = 128
COORD_STEPS = 16


full_turn = 6.283185307179586
step_size = 0.5
smooth_weight = 0.5


def extended(cells, sides, width):
    for axis, dim in sides:
        count = lax.axis_size(axis)
        ends = count - 1
        head = lax.slice_in_dim(cells, 0, width, axis=dim)
        tail = lax.slice_in_dim(cells, cells.shape[dim] - width, cells.shape[dim], axis=dim)
        cells = jnp.concatenate(
            [
                lax.ppermute(tail, axis, [(i, (i + 1) % count) for i in range(ends)]),
                cells,
                lax.ppermute(head, axis, [((i + 1) % count, i) for i in range(ends)]),
            ],
            axis=dim,
        )
    return cells


def receiver_lookup_dict(table_row, antenna_ids):
    numbers = jnp.arange(table_row.shape[0], dtype=jnp.int32)
    return jnp.sum(
        jnp.where(antenna_ids[:, None] == numbers[None, :], table_row[None, :], 0.0), axis=1
    )


def turns(coord, pixel, image):
    whole = jnp.round(coord * COORD_STEPS).astype(jnp.int32)
    rest = coord - whole.astype(jnp.float32) / COORD_STEPS
    period = COORD_STEPS * image
    exact = jnp.bitwise_and(whole[None, :] * pixel, period - 1).astype(jnp.float32) / period
    return exact + rest[None, :] * pixel.astype(jnp.float32) / image


def phase_table(coord, first_pixel, facet, image):
    blocks = facet // LANE_BLOCK
    starts = first_pixel[:, None] + LANE_BLOCK * jnp.arange(blocks, dtype=jnp.int32)[None, :]
    coarse = full_turn * turns(coord, starts.reshape(-1, 1), image)
    fine = full_turn * turns(coord, jnp.arange(LANE_BLOCK, dtype=jnp.int32)[:, None], image)
    coarse_c, coarse_s, fine_c, fine_s = lax.optimization_barrier(
        (jnp.cos(coarse), jnp.sin(coarse), jnp.cos(fine), jnp.sin(fine))
    )
    count = coord.shape[0]
    faces = first_pixel.shape[0]

    def spread(a):
        return jnp.broadcast_to(
            a.reshape(faces, blocks, 1, count), (faces, blocks, LANE_BLOCK, count)
        ).reshape(faces, facet, count)

    def tile(a):
        return jnp.broadcast_to(a[None, None], (faces, blocks, LANE_BLOCK, count)).reshape(
            faces, facet, count
        )

    pc, ps, qc, qs = spread(coarse_c), spread(coarse_s), tile(fine_c), tile(fine_s)
    return (pc * qc - ps * qs, ps * qc + pc * qs)


def local(
    patch_intensity,
    recorded_samples,
    sample_importance,
    block_populations,
    receiver_pairs,
    sample_rotation_phase,
    spectral_scaling,
    receiver_positions,
    patch_layout_position,
):
    rows_dev = patch_intensity.shape[0]
    ch_local = patch_intensity.shape[1]
    facets_here = patch_intensity.shape[2]
    facet = patch_intensity.shape[3]
    nvis = sample_importance.shape[0]
    n_vis = lax.axis_size("vis")
    image = GRID * facet
    norm_pred = 1.0 / math.sqrt(facets_here * facet * facet)
    norm_grad = 1.0 / math.sqrt(nvis * n_vis)
    eastward_shift = receiver_lookup_dict(
        receiver_positions[0], receiver_pairs[:, 0]
    ) - receiver_lookup_dict(receiver_positions[0], receiver_pairs[:, 1])
    northward_shift = receiver_lookup_dict(
        receiver_positions[1], receiver_pairs[:, 0]
    ) - receiver_lookup_dict(receiver_positions[1], receiver_pairs[:, 1])
    base_u = eastward_shift * jnp.cos(sample_rotation_phase) - northward_shift * jnp.sin(
        sample_rotation_phase
    )
    base_v = eastward_shift * jnp.sin(sample_rotation_phase) + northward_shift * jnp.cos(
        sample_rotation_phase
    )
    slots = jnp.arange(nvis, dtype=jnp.int32)
    block_of = slots // BLOCK
    block_numbers = jnp.arange(block_populations.shape[0], dtype=jnp.int32)
    block_count = jnp.sum(
        jnp.where(block_of[:, None] == block_numbers[None, :], block_populations[None, :], 0),
        axis=1,
    )
    scale_vis = (slots % BLOCK < block_count).astype(jnp.float32) * sample_importance
    sky_half = patch_intensity.astype(jnp.bfloat16)
    first_row = patch_layout_position[:, 0] * facet - image // 2
    first_col = patch_layout_position[:, 1] * facet - image // 2

    piece = lax.all_to_all(
        jnp.broadcast_to(sky_half[None], (n_vis,) + sky_half.shape).reshape(
            (n_vis * rows_dev,) + sky_half.shape[1:]
        ),
        "vis",
        0,
        0,
        tiled=True,
    )

    new_rows = []
    residuals = []
    for c in range(ch_local):
        coord_u = spectral_scaling[c] * base_u
        coord_v = spectral_scaling[c] * base_v
        row_cos, row_sin = phase_table(coord_u, first_row, facet, image)
        col_cos, col_sin = phase_table(coord_v, first_col, facet, image)
        cols = lax.optimization_barrier(
            jnp.concatenate([col_cos, col_sin], axis=2).astype(jnp.bfloat16)
        )
        sky_rows = jnp.transpose(piece[:, c], (1, 0, 2))
        waves = jnp.einsum("fij,fjk->fik", sky_rows, cols, preferred_element_type=jnp.float32)
        wave_c = waves[:, :, :nvis]
        wave_s = waves[:, :, nvis:]
        sum_re = jnp.sum(row_cos * wave_c - row_sin * wave_s, axis=(0, 1))
        sum_im = -jnp.sum(row_cos * wave_s + row_sin * wave_c, axis=(0, 1))
        resid_real = scale_vis * (norm_pred * sum_re - recorded_samples[c, 0])
        resid_imag = scale_vis * (norm_pred * sum_im - recorded_samples[c, 1])
        z_one = (row_cos * resid_real[None, None, :] - row_sin * resid_imag[None, None, :]).astype(
            jnp.bfloat16
        )
        z_two = (row_sin * resid_real[None, None, :] + row_cos * resid_imag[None, None, :]).astype(
            jnp.bfloat16
        )
        zs = jnp.concatenate([z_one, -z_two], axis=2)
        grad = jnp.einsum("fik,fjk->ifj", zs, cols, preferred_element_type=jnp.float32)
        new_rows.append(grad)
        residuals.append(jnp.stack([resid_real, resid_imag], axis=0))
    partial = jnp.stack(new_rows, axis=1)
    parts = lax.all_to_all(partial.astype(jnp.bfloat16), "vis", 0, 0, tiled=True)
    gradient = jnp.sum(
        parts.reshape((n_vis, rows_dev) + parts.shape[1:]).astype(jnp.float32), axis=0
    )
    padded = extended(patch_intensity.astype(jnp.bfloat16), (("chan", 1),), 1).astype(
        patch_intensity.dtype
    )
    left_side = padded[:, :-2]
    right_side = padded[:, 2:]
    chan_index = lax.axis_index("chan") * ch_local + jnp.arange(ch_local, dtype=jnp.int32)
    total_chan = ch_local * lax.axis_size("chan")
    has_left = (chan_index >= 1).astype(jnp.float32)[None, :, None, None]
    has_right = (chan_index <= total_chan - 2).astype(jnp.float32)[None, :, None, None]
    smooth = has_left * (patch_intensity - left_side) + has_right * (patch_intensity - right_side)
    new_sky = patch_intensity - step_size * (norm_grad * gradient + smooth_weight * smooth)
    residual = jnp.stack(residuals, axis=0)
    return (new_sky, residual)


def solution(mesh):
    return jax.shard_map(
        local,
        mesh=mesh,
        in_specs=(
            P("vis", "chan", None, None),
            P("chan", None, "vis"),
            P("vis"),
            P("vis"),
            P("vis", None),
            P("vis"),
            P("chan"),
            P(),
            P(),
        ),
        out_specs=(P("vis", "chan", None, None), P("chan", None, "vis")),
        check_vma=False,
    )
```

```python
import math

import jax
import jax.numpy as jnp
from jax import lax
from jax.sharding import PartitionSpec as P

GRID = 64
BLOCK = 256
LANE_BLOCK = 128
COORD_STEPS = 16


full_turn = 6.283185307179586
step_size = 0.5
smooth_weight = 0.5


def extended(cells, sides, width):
    for axis, dim in sides:
        count = lax.axis_size(axis)
        ends = count - 1
        head = lax.slice_in_dim(cells, 0, width, axis=dim)
        tail = lax.slice_in_dim(cells, cells.shape[dim] - width, cells.shape[dim], axis=dim)
        cells = jnp.concatenate(
            [
                lax.ppermute(tail, axis, [(i, (i + 1) % count) for i in range(ends)]),
                cells,
                lax.ppermute(head, axis, [((i + 1) % count, i) for i in range(ends)]),
            ],
            axis=dim,
        )
    return cells


def receiver_lookup_dict(table_row, antenna_ids):
    numbers = jnp.arange(table_row.shape[0], dtype=jnp.int32)
    return jnp.sum(
        jnp.where(antenna_ids[:, None] == numbers[None, :], table_row[None, :], 0.0), axis=1
    )


def turns(coord, pixel, image):
    whole = jnp.round(coord * COORD_STEPS).astype(jnp.int32)
    rest = coord - whole.astype(jnp.float32) / COORD_STEPS
    period = COORD_STEPS * image
    exact = jnp.bitwise_and(whole[None, :] * pixel, period - 1).astype(jnp.float32) / period
    return exact + rest[None, :] * pixel.astype(jnp.float32) / image


def phase_table(coord, first_pixel, facet, image):
    blocks = facet // LANE_BLOCK
    starts = first_pixel[:, None] + LANE_BLOCK * jnp.arange(blocks, dtype=jnp.int32)[None, :]
    coarse = full_turn * turns(coord, starts.reshape(-1, 1), image)
    fine = full_turn * turns(coord, jnp.arange(LANE_BLOCK, dtype=jnp.int32)[:, None], image)
    coarse_c, coarse_s, fine_c, fine_s = lax.optimization_barrier(
        (jnp.cos(coarse), jnp.sin(coarse), jnp.cos(fine), jnp.sin(fine))
    )
    count = coord.shape[0]
    faces = first_pixel.shape[0]

    def spread(a):
        return jnp.broadcast_to(
            a.reshape(faces, blocks, 1, count), (faces, blocks, LANE_BLOCK, count)
        ).reshape(faces, facet, count)

    def tile(a):
        return jnp.broadcast_to(a[None, None], (faces, blocks, LANE_BLOCK, count)).reshape(
            faces, facet, count
        )

    pc, ps, qc, qs = spread(coarse_c), spread(coarse_s), tile(fine_c), tile(fine_s)
    return (pc * qc - ps * qs, ps * qc + pc * qs)


def exchange(x, n_vis, mask):
    return lax.ppermute(x, "vis", [(i, i ^ mask) for i in range(n_vis)])


def gather_rows(block, n_vis):
    half = n_vis // 2
    me = lax.axis_index("vis")
    low = me % half
    other = exchange(block, n_vis, half)
    pair = jnp.where(me < half, jnp.stack([block, other]), jnp.stack([other, block]))
    pairs = jnp.stack([pair] + [exchange(pair, n_vis, m) for m in range(1, half)])
    order = jnp.bitwise_xor(jnp.arange(half, dtype=jnp.int32), low)
    full = jnp.take(pairs, order, axis=0)
    return jnp.swapaxes(full, 0, 1).reshape((n_vis * block.shape[0],) + block.shape[1:])


def reduce_rows(partial, n_vis, rows):
    half = n_vis // 2
    me = lax.axis_index("vis")
    low = me % half
    slabs = partial.astype(jnp.bfloat16).reshape((2, half, rows) + partial.shape[1:])
    order = jnp.bitwise_xor(jnp.arange(half, dtype=jnp.int32), low)
    slabs = jnp.take(slabs, order, axis=1)
    acc = slabs[:, 0].astype(jnp.float32)
    for m in range(1, half):
        acc = acc + exchange(slabs[:, m], n_vis, m).astype(jnp.float32)
    mine = jnp.where(me < half, acc[0], acc[1])
    send = jnp.where(me < half, acc[1], acc[0]).astype(jnp.bfloat16)
    return mine + exchange(send, n_vis, half).astype(jnp.float32)


def local(
    patch_intensity,
    recorded_samples,
    sample_importance,
    block_populations,
    receiver_pairs,
    sample_rotation_phase,
    spectral_scaling,
    receiver_positions,
    patch_layout_position,
):
    rows_dev = patch_intensity.shape[0]
    ch_local = patch_intensity.shape[1]
    facets_here = patch_intensity.shape[2]
    facet = patch_intensity.shape[3]
    nvis = sample_importance.shape[0]
    n_vis = lax.axis_size("vis")
    image = GRID * facet
    norm_pred = 1.0 / math.sqrt(facets_here * facet * facet)
    norm_grad = 1.0 / math.sqrt(nvis * n_vis)
    eastward_shift = receiver_lookup_dict(
        receiver_positions[0], receiver_pairs[:, 0]
    ) - receiver_lookup_dict(receiver_positions[0], receiver_pairs[:, 1])
    northward_shift = receiver_lookup_dict(
        receiver_positions[1], receiver_pairs[:, 0]
    ) - receiver_lookup_dict(receiver_positions[1], receiver_pairs[:, 1])
    base_u = eastward_shift * jnp.cos(sample_rotation_phase) - northward_shift * jnp.sin(
        sample_rotation_phase
    )
    base_v = eastward_shift * jnp.sin(sample_rotation_phase) + northward_shift * jnp.cos(
        sample_rotation_phase
    )
    slots = jnp.arange(nvis, dtype=jnp.int32)
    block_of = slots // BLOCK
    block_numbers = jnp.arange(block_populations.shape[0], dtype=jnp.int32)
    block_count = jnp.sum(
        jnp.where(block_of[:, None] == block_numbers[None, :], block_populations[None, :], 0),
        axis=1,
    )
    scale_vis = (slots % BLOCK < block_count).astype(jnp.float32) * sample_importance
    sky_half = patch_intensity.astype(jnp.bfloat16)
    first_row = patch_layout_position[:, 0] * facet - image // 2
    first_col = patch_layout_position[:, 1] * facet - image // 2

    piece = gather_rows(sky_half, n_vis)

    new_rows = []
    residuals = []
    for c in range(ch_local):
        coord_u = spectral_scaling[c] * base_u
        coord_v = spectral_scaling[c] * base_v
        row_cos, row_sin = phase_table(coord_u, first_row, facet, image)
        col_cos, col_sin = phase_table(coord_v, first_col, facet, image)
        cols = lax.optimization_barrier(
            jnp.concatenate([col_cos, col_sin], axis=2).astype(jnp.bfloat16)
        )
        sky_rows = jnp.transpose(piece[:, c], (1, 0, 2))
        waves = jnp.einsum("fij,fjk->fik", sky_rows, cols, preferred_element_type=jnp.float32)
        wave_c = waves[:, :, :nvis]
        wave_s = waves[:, :, nvis:]
        sum_re = jnp.sum(row_cos * wave_c - row_sin * wave_s, axis=(0, 1))
        sum_im = -jnp.sum(row_cos * wave_s + row_sin * wave_c, axis=(0, 1))
        resid_real = scale_vis * (norm_pred * sum_re - recorded_samples[c, 0])
        resid_imag = scale_vis * (norm_pred * sum_im - recorded_samples[c, 1])
        z_one = (row_cos * resid_real[None, None, :] - row_sin * resid_imag[None, None, :]).astype(
            jnp.bfloat16
        )
        z_two = (row_sin * resid_real[None, None, :] + row_cos * resid_imag[None, None, :]).astype(
            jnp.bfloat16
        )
        zs = jnp.concatenate([z_one, -z_two], axis=2)
        grad = jnp.einsum("fik,fjk->ifj", zs, cols, preferred_element_type=jnp.float32)
        new_rows.append(grad)
        residuals.append(jnp.stack([resid_real, resid_imag], axis=0))
    partial = jnp.stack(new_rows, axis=1)
    gradient = reduce_rows(partial, n_vis, rows_dev)
    padded = extended(patch_intensity.astype(jnp.bfloat16), (("chan", 1),), 1).astype(
        patch_intensity.dtype
    )
    left_side = padded[:, :-2]
    right_side = padded[:, 2:]
    chan_index = lax.axis_index("chan") * ch_local + jnp.arange(ch_local, dtype=jnp.int32)
    total_chan = ch_local * lax.axis_size("chan")
    has_left = (chan_index >= 1).astype(jnp.float32)[None, :, None, None]
    has_right = (chan_index <= total_chan - 2).astype(jnp.float32)[None, :, None, None]
    smooth = has_left * (patch_intensity - left_side) + has_right * (patch_intensity - right_side)
    new_sky = patch_intensity - step_size * (norm_grad * gradient + smooth_weight * smooth)
    residual = jnp.stack(residuals, axis=0)
    return (new_sky, residual)


def solution(mesh):
    return jax.shard_map(
        local,
        mesh=mesh,
        in_specs=(
            P("vis", "chan", None, None),
            P("chan", None, "vis"),
            P("vis"),
            P("vis"),
            P("vis", None),
            P("vis"),
            P("chan"),
            P(),
            P(),
        ),
        out_specs=(P("vis", "chan", None, None), P("chan", None, "vis")),
        check_vma=False,
    )
```

```python
import math

import jax
import jax.numpy as jnp
from jax import lax
from jax.sharding import PartitionSpec as P

GRID = 64
BLOCK = 256
LANE_BLOCK = 128
COORD_STEPS = 16


full_turn = 6.283185307179586
step_size = 0.5
smooth_weight = 0.5


def extended(cells, sides, width):
    for axis, dim in sides:
        count = lax.axis_size(axis)
        ends = count - 1
        head = lax.slice_in_dim(cells, 0, width, axis=dim)
        tail = lax.slice_in_dim(cells, cells.shape[dim] - width, cells.shape[dim], axis=dim)
        cells = jnp.concatenate(
            [
                lax.ppermute(tail, axis, [(i, (i + 1) % count) for i in range(ends)]),
                cells,
                lax.ppermute(head, axis, [((i + 1) % count, i) for i in range(ends)]),
            ],
            axis=dim,
        )
    return cells


def receiver_lookup_dict(table_row, antenna_ids):
    numbers = jnp.arange(table_row.shape[0], dtype=jnp.int32)
    return jnp.sum(
        jnp.where(antenna_ids[:, None] == numbers[None, :], table_row[None, :], 0.0), axis=1
    )


def turns(coord, pixel, image):
    whole = jnp.round(coord * COORD_STEPS).astype(jnp.int32)
    rest = coord - whole.astype(jnp.float32) / COORD_STEPS
    period = COORD_STEPS * image
    exact = jnp.bitwise_and(whole[None, :] * pixel, period - 1).astype(jnp.float32) / period
    return exact + rest[None, :] * pixel.astype(jnp.float32) / image


def phase_table(coord, first_pixel, facet, image):
    blocks = facet // LANE_BLOCK
    starts = first_pixel[:, None] + LANE_BLOCK * jnp.arange(blocks, dtype=jnp.int32)[None, :]
    coarse = full_turn * turns(coord, starts.reshape(-1, 1), image)
    fine = full_turn * turns(coord, jnp.arange(LANE_BLOCK, dtype=jnp.int32)[:, None], image)
    coarse_c, coarse_s, fine_c, fine_s = lax.optimization_barrier(
        (jnp.cos(coarse), jnp.sin(coarse), jnp.cos(fine), jnp.sin(fine))
    )
    count = coord.shape[0]
    faces = first_pixel.shape[0]

    def spread(a):
        return jnp.broadcast_to(
            a.reshape(faces, blocks, 1, count), (faces, blocks, LANE_BLOCK, count)
        ).reshape(faces, facet, count)

    def tile(a):
        return jnp.broadcast_to(a[None, None], (faces, blocks, LANE_BLOCK, count)).reshape(
            faces, facet, count
        )

    pc, ps, qc, qs = spread(coarse_c), spread(coarse_s), tile(fine_c), tile(fine_s)
    return (pc * qc - ps * qs, ps * qc + pc * qs)


def exchange(x, n_vis, mask):
    return lax.ppermute(x, "vis", [(i, i ^ mask) for i in range(n_vis)])


def gather_rows(block, n_vis):
    half = n_vis // 2
    me = lax.axis_index("vis")
    low = me % half
    other = exchange(block, n_vis, half)
    pair = jnp.where(me < half, jnp.stack([block, other]), jnp.stack([other, block]))
    groups = [list(range(half)), list(range(half, n_vis))]
    full = lax.all_to_all(
        jnp.broadcast_to(pair[None], (half,) + pair.shape), "vis", 0, 0, axis_index_groups=groups
    )
    return jnp.swapaxes(full, 0, 1).reshape((n_vis * block.shape[0],) + block.shape[1:])


def reduce_rows(partial, n_vis, rows):
    half = n_vis // 2
    me = lax.axis_index("vis")
    low = me % half
    slabs = partial.astype(jnp.bfloat16).reshape((2, half, rows) + partial.shape[1:])
    groups = [list(range(half)), list(range(half, n_vis))]
    got = lax.all_to_all(jnp.swapaxes(slabs, 0, 1), "vis", 0, 0, axis_index_groups=groups)
    acc = jnp.sum(got.astype(jnp.float32), axis=0)
    mine = jnp.where(me < half, acc[0], acc[1])
    send = jnp.where(me < half, acc[1], acc[0]).astype(jnp.bfloat16)
    return mine + exchange(send, n_vis, half).astype(jnp.float32)


def local(
    patch_intensity,
    recorded_samples,
    sample_importance,
    block_populations,
    receiver_pairs,
    sample_rotation_phase,
    spectral_scaling,
    receiver_positions,
    patch_layout_position,
):
    rows_dev = patch_intensity.shape[0]
    ch_local = patch_intensity.shape[1]
    facets_here = patch_intensity.shape[2]
    facet = patch_intensity.shape[3]
    nvis = sample_importance.shape[0]
    n_vis = lax.axis_size("vis")
    image = GRID * facet
    norm_pred = 1.0 / math.sqrt(facets_here * facet * facet)
    norm_grad = 1.0 / math.sqrt(nvis * n_vis)
    eastward_shift = receiver_lookup_dict(
        receiver_positions[0], receiver_pairs[:, 0]
    ) - receiver_lookup_dict(receiver_positions[0], receiver_pairs[:, 1])
    northward_shift = receiver_lookup_dict(
        receiver_positions[1], receiver_pairs[:, 0]
    ) - receiver_lookup_dict(receiver_positions[1], receiver_pairs[:, 1])
    base_u = eastward_shift * jnp.cos(sample_rotation_phase) - northward_shift * jnp.sin(
        sample_rotation_phase
    )
    base_v = eastward_shift * jnp.sin(sample_rotation_phase) + northward_shift * jnp.cos(
        sample_rotation_phase
    )
    slots = jnp.arange(nvis, dtype=jnp.int32)
    block_of = slots // BLOCK
    block_numbers = jnp.arange(block_populations.shape[0], dtype=jnp.int32)
    block_count = jnp.sum(
        jnp.where(block_of[:, None] == block_numbers[None, :], block_populations[None, :], 0),
        axis=1,
    )
    scale_vis = (slots % BLOCK < block_count).astype(jnp.float32) * sample_importance
    sky_half = patch_intensity.astype(jnp.bfloat16)
    first_row = patch_layout_position[:, 0] * facet - image // 2
    first_col = patch_layout_position[:, 1] * facet - image // 2

    piece = gather_rows(sky_half, n_vis)

    new_rows = []
    residuals = []
    for c in range(ch_local):
        coord_u = spectral_scaling[c] * base_u
        coord_v = spectral_scaling[c] * base_v
        row_cos, row_sin = phase_table(coord_u, first_row, facet, image)
        col_cos, col_sin = phase_table(coord_v, first_col, facet, image)
        cols = lax.optimization_barrier(
            jnp.concatenate([col_cos, col_sin], axis=2).astype(jnp.bfloat16)
        )
        sky_rows = jnp.transpose(piece[:, c], (1, 0, 2))
        waves = jnp.einsum("fij,fjk->fik", sky_rows, cols, preferred_element_type=jnp.float32)
        wave_c = waves[:, :, :nvis]
        wave_s = waves[:, :, nvis:]
        sum_re = jnp.sum(row_cos * wave_c - row_sin * wave_s, axis=(0, 1))
        sum_im = -jnp.sum(row_cos * wave_s + row_sin * wave_c, axis=(0, 1))
        resid_real = scale_vis * (norm_pred * sum_re - recorded_samples[c, 0])
        resid_imag = scale_vis * (norm_pred * sum_im - recorded_samples[c, 1])
        z_one = (row_cos * resid_real[None, None, :] - row_sin * resid_imag[None, None, :]).astype(
            jnp.bfloat16
        )
        z_two = (row_sin * resid_real[None, None, :] + row_cos * resid_imag[None, None, :]).astype(
            jnp.bfloat16
        )
        zs = jnp.concatenate([z_one, -z_two], axis=2)
        grad = jnp.einsum("fik,fjk->ifj", zs, cols, preferred_element_type=jnp.float32)
        new_rows.append(grad)
        residuals.append(jnp.stack([resid_real, resid_imag], axis=0))
    partial = jnp.stack(new_rows, axis=1)
    gradient = reduce_rows(partial, n_vis, rows_dev)
    padded = extended(patch_intensity.astype(jnp.bfloat16), (("chan", 1),), 1).astype(
        patch_intensity.dtype
    )
    left_side = padded[:, :-2]
    right_side = padded[:, 2:]
    chan_index = lax.axis_index("chan") * ch_local + jnp.arange(ch_local, dtype=jnp.int32)
    total_chan = ch_local * lax.axis_size("chan")
    has_left = (chan_index >= 1).astype(jnp.float32)[None, :, None, None]
    has_right = (chan_index <= total_chan - 2).astype(jnp.float32)[None, :, None, None]
    smooth = has_left * (patch_intensity - left_side) + has_right * (patch_intensity - right_side)
    new_sky = patch_intensity - step_size * (norm_grad * gradient + smooth_weight * smooth)
    residual = jnp.stack(residuals, axis=0)
    return (new_sky, residual)


def solution(mesh):
    return jax.shard_map(
        local,
        mesh=mesh,
        in_specs=(
            P("vis", "chan", None, None),
            P("chan", None, "vis"),
            P("vis"),
            P("vis"),
            P("vis", None),
            P("vis"),
            P("chan"),
            P(),
            P(),
        ),
        out_specs=(P("vis", "chan", None, None), P("chan", None, "vis")),
        check_vma=False,
    )
```

```python
import math

import jax
import jax.numpy as jnp
from jax import lax
from jax.sharding import PartitionSpec as P

GRID = 64
BLOCK = 256
LANE_BLOCK = 128
COORD_STEPS = 16


full_turn = 6.283185307179586
step_size = 0.5
smooth_weight = 0.5


def extended(cells, sides, width):
    for axis, dim in sides:
        count = lax.axis_size(axis)
        ends = count - 1
        head = lax.slice_in_dim(cells, 0, width, axis=dim)
        tail = lax.slice_in_dim(cells, cells.shape[dim] - width, cells.shape[dim], axis=dim)
        cells = jnp.concatenate(
            [
                lax.ppermute(tail, axis, [(i, (i + 1) % count) for i in range(ends)]),
                cells,
                lax.ppermute(head, axis, [((i + 1) % count, i) for i in range(ends)]),
            ],
            axis=dim,
        )
    return cells


def receiver_lookup_dict(table_row, antenna_ids):
    numbers = jnp.arange(table_row.shape[0], dtype=jnp.int32)
    return jnp.sum(
        jnp.where(antenna_ids[:, None] == numbers[None, :], table_row[None, :], 0.0), axis=1
    )


def turns(coord, pixel, image):
    whole = jnp.round(coord * COORD_STEPS).astype(jnp.int32)
    rest = coord - whole.astype(jnp.float32) / COORD_STEPS
    period = COORD_STEPS * image
    exact = jnp.bitwise_and(whole[None, :] * pixel, period - 1).astype(jnp.float32) / period
    return exact + rest[None, :] * pixel.astype(jnp.float32) / image


def phase_table(coord, starts, span, image):
    faces, chunks = starts.shape
    coarse = full_turn * turns(coord, starts.reshape(-1, 1), image)
    fine = full_turn * turns(coord, jnp.arange(span, dtype=jnp.int32)[:, None], image)
    coarse_c, coarse_s, fine_c, fine_s = lax.optimization_barrier(
        (jnp.cos(coarse), jnp.sin(coarse), jnp.cos(fine), jnp.sin(fine))
    )
    count = coord.shape[0]

    def spread(a):
        return jnp.broadcast_to(
            a.reshape(faces, chunks, 1, count), (faces, chunks, span, count)
        ).reshape(faces, chunks * span, count)

    def tile(a):
        return jnp.broadcast_to(a[None, None], (faces, chunks, span, count)).reshape(
            faces, chunks * span, count
        )

    pc, ps, qc, qs = spread(coarse_c), spread(coarse_s), tile(fine_c), tile(fine_s)
    return (pc * qc - ps * qs, ps * qc + pc * qs)


def exchange(x, n_vis, mask):
    return lax.ppermute(x, "vis", [(i, i ^ mask) for i in range(n_vis)])


def gather_rows(block, n_vis):
    half = n_vis // 2
    me = lax.axis_index("vis")
    other = exchange(block, n_vis, half)
    pair = jnp.where(me < half, jnp.stack([block, other]), jnp.stack([other, block]))
    groups = [list(range(half)), list(range(half, n_vis))]
    full = lax.all_to_all(
        jnp.broadcast_to(pair[None], (half,) + pair.shape), "vis", 0, 0, axis_index_groups=groups
    )
    return full.reshape((n_vis * block.shape[0],) + block.shape[1:])


def reduce_rows(partial, n_vis, rows):
    half = n_vis // 2
    me = lax.axis_index("vis")
    slabs = partial.astype(jnp.bfloat16).reshape((half, 2, rows) + partial.shape[1:])
    groups = [list(range(half)), list(range(half, n_vis))]
    got = lax.all_to_all(slabs, "vis", 0, 0, axis_index_groups=groups)
    acc = jnp.sum(got.astype(jnp.float32), axis=0)
    mine = jnp.where(me < half, acc[0], acc[1])
    send = jnp.where(me < half, acc[1], acc[0]).astype(jnp.bfloat16)
    return mine + exchange(send, n_vis, half).astype(jnp.float32)


def local(
    patch_intensity,
    recorded_samples,
    sample_importance,
    block_populations,
    receiver_pairs,
    sample_rotation_phase,
    spectral_scaling,
    receiver_positions,
    patch_layout_position,
):
    rows_dev = patch_intensity.shape[0]
    ch_local = patch_intensity.shape[1]
    facets_here = patch_intensity.shape[2]
    facet = patch_intensity.shape[3]
    nvis = sample_importance.shape[0]
    n_vis = lax.axis_size("vis")
    image = GRID * facet
    norm_pred = 1.0 / math.sqrt(facets_here * facet * facet)
    norm_grad = 1.0 / math.sqrt(nvis * n_vis)
    eastward_shift = receiver_lookup_dict(
        receiver_positions[0], receiver_pairs[:, 0]
    ) - receiver_lookup_dict(receiver_positions[0], receiver_pairs[:, 1])
    northward_shift = receiver_lookup_dict(
        receiver_positions[1], receiver_pairs[:, 0]
    ) - receiver_lookup_dict(receiver_positions[1], receiver_pairs[:, 1])
    base_u = eastward_shift * jnp.cos(sample_rotation_phase) - northward_shift * jnp.sin(
        sample_rotation_phase
    )
    base_v = eastward_shift * jnp.sin(sample_rotation_phase) + northward_shift * jnp.cos(
        sample_rotation_phase
    )
    slots = jnp.arange(nvis, dtype=jnp.int32)
    block_of = slots // BLOCK
    block_numbers = jnp.arange(block_populations.shape[0], dtype=jnp.int32)
    block_count = jnp.sum(
        jnp.where(block_of[:, None] == block_numbers[None, :], block_populations[None, :], 0),
        axis=1,
    )
    scale_vis = (slots % BLOCK < block_count).astype(jnp.float32) * sample_importance
    sky_half = patch_intensity.astype(jnp.bfloat16)
    first_row = patch_layout_position[:, 0] * facet - image // 2
    first_col = patch_layout_position[:, 1] * facet - image // 2
    chunk = jnp.arange(n_vis, dtype=jnp.int32)
    owner = (chunk % 2) * (n_vis // 2) + chunk // 2
    row_starts = first_row[:, None] + rows_dev * owner[None, :]
    col_starts = first_col[:, None] + LANE_BLOCK * jnp.arange(facet // LANE_BLOCK, dtype=jnp.int32)

    piece = gather_rows(sky_half, n_vis)

    new_rows = []
    residuals = []
    for c in range(ch_local):
        coord_u = spectral_scaling[c] * base_u
        coord_v = spectral_scaling[c] * base_v
        row_cos, row_sin = phase_table(coord_u, row_starts, rows_dev, image)
        col_cos, col_sin = phase_table(coord_v, col_starts, LANE_BLOCK, image)
        cols = lax.optimization_barrier(
            jnp.concatenate([col_cos, col_sin], axis=2).astype(jnp.bfloat16)
        )
        sky_rows = jnp.transpose(piece[:, c], (1, 0, 2))
        waves = jnp.einsum("fij,fjk->fik", sky_rows, cols, preferred_element_type=jnp.float32)
        wave_c = waves[:, :, :nvis]
        wave_s = waves[:, :, nvis:]
        sum_re = jnp.sum(row_cos * wave_c - row_sin * wave_s, axis=(0, 1))
        sum_im = -jnp.sum(row_cos * wave_s + row_sin * wave_c, axis=(0, 1))
        resid_real = scale_vis * (norm_pred * sum_re - recorded_samples[c, 0])
        resid_imag = scale_vis * (norm_pred * sum_im - recorded_samples[c, 1])
        z_one = (row_cos * resid_real[None, None, :] - row_sin * resid_imag[None, None, :]).astype(
            jnp.bfloat16
        )
        z_two = (row_sin * resid_real[None, None, :] + row_cos * resid_imag[None, None, :]).astype(
            jnp.bfloat16
        )
        zs = jnp.concatenate([z_one, -z_two], axis=2)
        grad = jnp.einsum("fik,fjk->ifj", zs, cols, preferred_element_type=jnp.float32)
        new_rows.append(grad)
        residuals.append(jnp.stack([resid_real, resid_imag], axis=0))
    partial = jnp.stack(new_rows, axis=1)
    gradient = reduce_rows(partial, n_vis, rows_dev)
    padded = extended(patch_intensity.astype(jnp.bfloat16), (("chan", 1),), 1).astype(
        patch_intensity.dtype
    )
    left_side = padded[:, :-2]
    right_side = padded[:, 2:]
    chan_index = lax.axis_index("chan") * ch_local + jnp.arange(ch_local, dtype=jnp.int32)
    total_chan = ch_local * lax.axis_size("chan")
    has_left = (chan_index >= 1).astype(jnp.float32)[None, :, None, None]
    has_right = (chan_index <= total_chan - 2).astype(jnp.float32)[None, :, None, None]
    smooth = has_left * (patch_intensity - left_side) + has_right * (patch_intensity - right_side)
    new_sky = patch_intensity - step_size * (norm_grad * gradient + smooth_weight * smooth)
    residual = jnp.stack(residuals, axis=0)
    return (new_sky, residual)


def solution(mesh):
    return jax.shard_map(
        local,
        mesh=mesh,
        in_specs=(
            P("vis", "chan", None, None),
            P("chan", None, "vis"),
            P("vis"),
            P("vis"),
            P("vis", None),
            P("vis"),
            P("chan"),
            P(),
            P(),
        ),
        out_specs=(P("vis", "chan", None, None), P("chan", None, "vis")),
        check_vma=False,
    )
```

```python
import math

import jax
import jax.numpy as jnp
from jax import lax
from jax.sharding import PartitionSpec as P

GRID = 64
BLOCK = 256
LANE_BLOCK = 128
COORD_STEPS = 16


full_turn = 6.283185307179586
step_size = 0.5
smooth_weight = 0.5


def extended(cells, sides, width):
    for axis, dim in sides:
        count = lax.axis_size(axis)
        ends = count - 1
        head = lax.slice_in_dim(cells, 0, width, axis=dim)
        tail = lax.slice_in_dim(cells, cells.shape[dim] - width, cells.shape[dim], axis=dim)
        cells = jnp.concatenate(
            [
                lax.ppermute(tail, axis, [(i, (i + 1) % count) for i in range(ends)]),
                cells,
                lax.ppermute(head, axis, [((i + 1) % count, i) for i in range(ends)]),
            ],
            axis=dim,
        )
    return cells


def receiver_lookup_dict(table_row, antenna_ids):
    numbers = jnp.arange(table_row.shape[0], dtype=jnp.int32)
    return jnp.sum(
        jnp.where(antenna_ids[:, None] == numbers[None, :], table_row[None, :], 0.0), axis=1
    )


def turns(coord, pixel, image):
    whole = jnp.round(coord * COORD_STEPS).astype(jnp.int32)
    rest = coord - whole.astype(jnp.float32) / COORD_STEPS
    period = COORD_STEPS * image
    exact = jnp.bitwise_and(whole[None, :] * pixel, period - 1).astype(jnp.float32) / period
    return exact + rest[None, :] * pixel.astype(jnp.float32) / image


def phase_table(coord, starts, span, image):
    faces, chunks = starts.shape
    coarse = full_turn * turns(coord, starts.reshape(-1, 1), image)
    fine = full_turn * turns(coord, jnp.arange(span, dtype=jnp.int32)[:, None], image)
    coarse_c, coarse_s, fine_c, fine_s = lax.optimization_barrier(
        (jnp.cos(coarse), jnp.sin(coarse), jnp.cos(fine), jnp.sin(fine))
    )
    count = coord.shape[0]

    def spread(a):
        return jnp.broadcast_to(
            a.reshape(faces, chunks, 1, count), (faces, chunks, span, count)
        ).reshape(faces, chunks * span, count)

    def tile(a):
        return jnp.broadcast_to(a[None, None], (faces, chunks, span, count)).reshape(
            faces, chunks * span, count
        )

    pc, ps, qc, qs = spread(coarse_c), spread(coarse_s), tile(fine_c), tile(fine_s)
    return (pc * qc - ps * qs, ps * qc + pc * qs)


def exchange(x, n_vis, mask):
    return lax.ppermute(x, "vis", [(i, i ^ mask) for i in range(n_vis)])


def gather_rows(block, n_vis):
    half = n_vis // 2
    me = lax.axis_index("vis")
    other = exchange(block, n_vis, half)
    pair = jnp.where(me < half, jnp.stack([block, other]), jnp.stack([other, block]))
    groups = [list(range(half)), list(range(half, n_vis))]
    full = lax.all_to_all(
        jnp.broadcast_to(pair[None], (half,) + pair.shape), "vis", 0, 0, axis_index_groups=groups
    )
    return full.reshape((n_vis * block.shape[0],) + block.shape[1:])


def reduce_rows(partial, n_vis, rows):
    half = n_vis // 2
    me = lax.axis_index("vis")
    slabs = partial.astype(jnp.bfloat16).reshape((half, 2, rows) + partial.shape[1:])
    groups = [list(range(half)), list(range(half, n_vis))]
    got = lax.all_to_all(slabs, "vis", 0, 0, axis_index_groups=groups)
    acc = jnp.sum(got.astype(jnp.float32), axis=0)
    mine = jnp.where(me < half, acc[0], acc[1])
    send = jnp.where(me < half, acc[1], acc[0]).astype(jnp.bfloat16)
    return mine + exchange(send, n_vis, half).astype(jnp.float32)


def local(
    patch_intensity,
    recorded_samples,
    sample_importance,
    block_populations,
    receiver_pairs,
    sample_rotation_phase,
    spectral_scaling,
    receiver_positions,
    patch_layout_position,
):
    rows_dev = patch_intensity.shape[0]
    ch_local = patch_intensity.shape[1]
    facets_here = patch_intensity.shape[2]
    facet = patch_intensity.shape[3]
    nvis = sample_importance.shape[0]
    n_vis = lax.axis_size("vis")
    image = GRID * facet
    norm_pred = 1.0 / math.sqrt(facets_here * facet * facet)
    norm_grad = 1.0 / math.sqrt(nvis * n_vis)
    eastward_shift = receiver_lookup_dict(
        receiver_positions[0], receiver_pairs[:, 0]
    ) - receiver_lookup_dict(receiver_positions[0], receiver_pairs[:, 1])
    northward_shift = receiver_lookup_dict(
        receiver_positions[1], receiver_pairs[:, 0]
    ) - receiver_lookup_dict(receiver_positions[1], receiver_pairs[:, 1])
    base_u = eastward_shift * jnp.cos(sample_rotation_phase) - northward_shift * jnp.sin(
        sample_rotation_phase
    )
    base_v = eastward_shift * jnp.sin(sample_rotation_phase) + northward_shift * jnp.cos(
        sample_rotation_phase
    )
    slots = jnp.arange(nvis, dtype=jnp.int32)
    block_of = slots // BLOCK
    block_numbers = jnp.arange(block_populations.shape[0], dtype=jnp.int32)
    block_count = jnp.sum(
        jnp.where(block_of[:, None] == block_numbers[None, :], block_populations[None, :], 0),
        axis=1,
    )
    scale_vis = (slots % BLOCK < block_count).astype(jnp.float32) * sample_importance
    sky_half = patch_intensity.astype(jnp.bfloat16)
    first_row = patch_layout_position[:, 0] * facet - image // 2
    first_col = patch_layout_position[:, 1] * facet - image // 2
    chunk = jnp.arange(n_vis, dtype=jnp.int32)
    owner = (chunk % 2) * (n_vis // 2) + chunk // 2
    row_starts = first_row[:, None] + rows_dev * owner[None, :]
    col_starts = first_col[:, None] + LANE_BLOCK * jnp.arange(facet // LANE_BLOCK, dtype=jnp.int32)

    piece = gather_rows(sky_half, n_vis)

    new_rows = []
    residuals = []
    for c in range(ch_local):
        coord_u = spectral_scaling[c] * base_u
        coord_v = spectral_scaling[c] * base_v
        row_cos, row_sin = phase_table(coord_u, row_starts, rows_dev, image)
        col_cos, col_sin = phase_table(coord_v, col_starts, LANE_BLOCK, image)
        cols = lax.optimization_barrier(
            jnp.concatenate([col_cos, col_sin], axis=2).astype(jnp.bfloat16)
        )
        sky_rows = jnp.transpose(piece[:, c], (1, 0, 2))
        waves = lax.optimization_barrier(jnp.einsum("fij,fjk->fik", sky_rows, cols, preferred_element_type=jnp.bfloat16)).astype(jnp.float32)
        wave_c = waves[:, :, :nvis]
        wave_s = waves[:, :, nvis:]
        sum_re = jnp.sum(row_cos * wave_c - row_sin * wave_s, axis=(0, 1))
        sum_im = -jnp.sum(row_cos * wave_s + row_sin * wave_c, axis=(0, 1))
        resid_real = scale_vis * (norm_pred * sum_re - recorded_samples[c, 0])
        resid_imag = scale_vis * (norm_pred * sum_im - recorded_samples[c, 1])
        z_one = (row_cos * resid_real[None, None, :] - row_sin * resid_imag[None, None, :]).astype(
            jnp.bfloat16
        )
        z_two = (row_sin * resid_real[None, None, :] + row_cos * resid_imag[None, None, :]).astype(
            jnp.bfloat16
        )
        zs = jnp.concatenate([z_one, -z_two], axis=2)
        grad = jnp.einsum("fik,fjk->ifj", zs, cols, preferred_element_type=jnp.float32)
        new_rows.append(grad)
        residuals.append(jnp.stack([resid_real, resid_imag], axis=0))
    partial = jnp.stack(new_rows, axis=1)
    gradient = reduce_rows(partial, n_vis, rows_dev)
    padded = extended(patch_intensity.astype(jnp.bfloat16), (("chan", 1),), 1).astype(
        patch_intensity.dtype
    )
    left_side = padded[:, :-2]
    right_side = padded[:, 2:]
    chan_index = lax.axis_index("chan") * ch_local + jnp.arange(ch_local, dtype=jnp.int32)
    total_chan = ch_local * lax.axis_size("chan")
    has_left = (chan_index >= 1).astype(jnp.float32)[None, :, None, None]
    has_right = (chan_index <= total_chan - 2).astype(jnp.float32)[None, :, None, None]
    smooth = has_left * (patch_intensity - left_side) + has_right * (patch_intensity - right_side)
    new_sky = patch_intensity - step_size * (norm_grad * gradient + smooth_weight * smooth)
    residual = jnp.stack(residuals, axis=0)
    return (new_sky, residual)


def solution(mesh):
    return jax.shard_map(
        local,
        mesh=mesh,
        in_specs=(
            P("vis", "chan", None, None),
            P("chan", None, "vis"),
            P("vis"),
            P("vis"),
            P("vis", None),
            P("vis"),
            P("chan"),
            P(),
            P(),
        ),
        out_specs=(P("vis", "chan", None, None), P("chan", None, "vis")),
        check_vma=False,
    )
```

```python
import math

import jax
import jax.numpy as jnp
from jax import lax
from jax.sharding import PartitionSpec as P

GRID = 64
BLOCK = 256
LANE_BLOCK = 128
COORD_STEPS = 16


full_turn = 6.283185307179586
step_size = 0.5
smooth_weight = 0.5


def extended(cells, sides, width):
    for axis, dim in sides:
        count = lax.axis_size(axis)
        ends = count - 1
        head = lax.slice_in_dim(cells, 0, width, axis=dim)
        tail = lax.slice_in_dim(cells, cells.shape[dim] - width, cells.shape[dim], axis=dim)
        cells = jnp.concatenate(
            [
                lax.ppermute(tail, axis, [(i, (i + 1) % count) for i in range(ends)]),
                cells,
                lax.ppermute(head, axis, [((i + 1) % count, i) for i in range(ends)]),
            ],
            axis=dim,
        )
    return cells


def receiver_lookup_dict(table_row, antenna_ids):
    numbers = jnp.arange(table_row.shape[0], dtype=jnp.int32)
    return jnp.sum(
        jnp.where(antenna_ids[:, None] == numbers[None, :], table_row[None, :], 0.0), axis=1
    )


def turns(coord, pixel, image):
    whole = jnp.round(coord * COORD_STEPS).astype(jnp.int32)
    rest = coord - whole.astype(jnp.float32) / COORD_STEPS
    period = COORD_STEPS * image
    exact = jnp.bitwise_and(whole[None, :] * pixel, period - 1).astype(jnp.float32) / period
    return exact + rest[None, :] * pixel.astype(jnp.float32) / image


def phase_table(coord, starts, span, image):
    faces, chunks = starts.shape
    coarse = full_turn * turns(coord, starts.reshape(-1, 1), image)
    fine = full_turn * turns(coord, jnp.arange(span, dtype=jnp.int32)[:, None], image)
    coarse_c, coarse_s, fine_c, fine_s = lax.optimization_barrier(
        (jnp.cos(coarse), jnp.sin(coarse), jnp.cos(fine), jnp.sin(fine))
    )
    count = coord.shape[0]

    def spread(a):
        return jnp.broadcast_to(
            a.reshape(faces, chunks, 1, count), (faces, chunks, span, count)
        ).reshape(faces, chunks * span, count)

    def tile(a):
        return jnp.broadcast_to(a[None, None], (faces, chunks, span, count)).reshape(
            faces, chunks * span, count
        )

    pc, ps, qc, qs = spread(coarse_c), spread(coarse_s), tile(fine_c), tile(fine_s)
    return (pc * qc - ps * qs, ps * qc + pc * qs)


def exchange(x, n_vis, mask):
    return lax.ppermute(x, "vis", [(i, i ^ mask) for i in range(n_vis)])


def gather_rows(block, n_vis):
    half = n_vis // 2
    me = lax.axis_index("vis")
    other = exchange(block, n_vis, half)
    pair = jnp.where(me < half, jnp.stack([block, other]), jnp.stack([other, block]))
    groups = [list(range(half)), list(range(half, n_vis))]
    full = lax.all_to_all(
        jnp.broadcast_to(pair[None], (half,) + pair.shape), "vis", 0, 0, axis_index_groups=groups
    )
    return full.reshape((n_vis * block.shape[0],) + block.shape[1:])


def reduce_rows(partial, n_vis, rows):
    half = n_vis // 2
    me = lax.axis_index("vis")
    slabs = partial.astype(jnp.bfloat16).reshape((half, 2, rows) + partial.shape[1:])
    groups = [list(range(half)), list(range(half, n_vis))]
    got = lax.all_to_all(slabs, "vis", 0, 0, axis_index_groups=groups)
    acc = jnp.sum(got.astype(jnp.float32), axis=0)
    mine = jnp.where(me < half, acc[0], acc[1])
    send = jnp.where(me < half, acc[1], acc[0]).astype(jnp.bfloat16)
    return mine + exchange(send, n_vis, half).astype(jnp.float32)


def local(
    patch_intensity,
    recorded_samples,
    sample_importance,
    block_populations,
    receiver_pairs,
    sample_rotation_phase,
    spectral_scaling,
    receiver_positions,
    patch_layout_position,
):
    rows_dev = patch_intensity.shape[0]
    ch_local = patch_intensity.shape[1]
    facets_here = patch_intensity.shape[2]
    facet = patch_intensity.shape[3]
    nvis = sample_importance.shape[0]
    n_vis = lax.axis_size("vis")
    image = GRID * facet
    norm_pred = 1.0 / math.sqrt(facets_here * facet * facet)
    norm_grad = 1.0 / math.sqrt(nvis * n_vis)
    eastward_shift = receiver_lookup_dict(
        receiver_positions[0], receiver_pairs[:, 0]
    ) - receiver_lookup_dict(receiver_positions[0], receiver_pairs[:, 1])
    northward_shift = receiver_lookup_dict(
        receiver_positions[1], receiver_pairs[:, 0]
    ) - receiver_lookup_dict(receiver_positions[1], receiver_pairs[:, 1])
    base_u = eastward_shift * jnp.cos(sample_rotation_phase) - northward_shift * jnp.sin(
        sample_rotation_phase
    )
    base_v = eastward_shift * jnp.sin(sample_rotation_phase) + northward_shift * jnp.cos(
        sample_rotation_phase
    )
    slots = jnp.arange(nvis, dtype=jnp.int32)
    block_of = slots // BLOCK
    block_numbers = jnp.arange(block_populations.shape[0], dtype=jnp.int32)
    block_count = jnp.sum(
        jnp.where(block_of[:, None] == block_numbers[None, :], block_populations[None, :], 0),
        axis=1,
    )
    scale_vis = (slots % BLOCK < block_count).astype(jnp.float32) * sample_importance
    sky_half = patch_intensity.astype(jnp.bfloat16)
    first_row = patch_layout_position[:, 0] * facet - image // 2
    first_col = patch_layout_position[:, 1] * facet - image // 2
    chunk = jnp.arange(n_vis, dtype=jnp.int32)
    owner = (chunk % 2) * (n_vis // 2) + chunk // 2
    row_starts = first_row[:, None] + rows_dev * owner[None, :]
    col_starts = first_col[:, None] + LANE_BLOCK * jnp.arange(facet // LANE_BLOCK, dtype=jnp.int32)

    piece = gather_rows(sky_half, n_vis)

    new_rows = []
    residuals = []
    for c in range(ch_local):
        coord_u = spectral_scaling[c] * base_u
        coord_v = spectral_scaling[c] * base_v
        row_cos, row_sin = phase_table(coord_u, row_starts, rows_dev, image)
        col_cos, col_sin = phase_table(coord_v, col_starts, LANE_BLOCK, image)
        cols = lax.optimization_barrier(
            jnp.swapaxes(jnp.concatenate([col_cos, col_sin], axis=2), 1, 2).astype(jnp.bfloat16)
        )
        sky_rows = jnp.transpose(piece[:, c], (1, 0, 2))
        waves = jnp.einsum("fij,fkj->fik", sky_rows, cols, preferred_element_type=jnp.float32)
        wave_c = waves[:, :, :nvis]
        wave_s = waves[:, :, nvis:]
        sum_re = jnp.sum(row_cos * wave_c - row_sin * wave_s, axis=(0, 1))
        sum_im = -jnp.sum(row_cos * wave_s + row_sin * wave_c, axis=(0, 1))
        resid_real = scale_vis * (norm_pred * sum_re - recorded_samples[c, 0])
        resid_imag = scale_vis * (norm_pred * sum_im - recorded_samples[c, 1])
        z_one = (row_cos * resid_real[None, None, :] - row_sin * resid_imag[None, None, :]).astype(
            jnp.bfloat16
        )
        z_two = (row_sin * resid_real[None, None, :] + row_cos * resid_imag[None, None, :]).astype(
            jnp.bfloat16
        )
        zs = jnp.concatenate([z_one, -z_two], axis=2)
        grad = jnp.einsum("fik,fkj->ifj", zs, cols, preferred_element_type=jnp.float32)
        new_rows.append(grad)
        residuals.append(jnp.stack([resid_real, resid_imag], axis=0))
    partial = jnp.stack(new_rows, axis=1)
    gradient = reduce_rows(partial, n_vis, rows_dev)
    padded = extended(patch_intensity.astype(jnp.bfloat16), (("chan", 1),), 1).astype(
        patch_intensity.dtype
    )
    left_side = padded[:, :-2]
    right_side = padded[:, 2:]
    chan_index = lax.axis_index("chan") * ch_local + jnp.arange(ch_local, dtype=jnp.int32)
    total_chan = ch_local * lax.axis_size("chan")
    has_left = (chan_index >= 1).astype(jnp.float32)[None, :, None, None]
    has_right = (chan_index <= total_chan - 2).astype(jnp.float32)[None, :, None, None]
    smooth = has_left * (patch_intensity - left_side) + has_right * (patch_intensity - right_side)
    new_sky = patch_intensity - step_size * (norm_grad * gradient + smooth_weight * smooth)
    residual = jnp.stack(residuals, axis=0)
    return (new_sky, residual)


def solution(mesh):
    return jax.shard_map(
        local,
        mesh=mesh,
        in_specs=(
            P("vis", "chan", None, None),
            P("chan", None, "vis"),
            P("vis"),
            P("vis"),
            P("vis", None),
            P("vis"),
            P("chan"),
            P(),
            P(),
        ),
        out_specs=(P("vis", "chan", None, None), P("chan", None, "vis")),
        check_vma=False,
    )
```

```python
import math

import jax
import jax.numpy as jnp
from jax import lax
from jax.sharding import PartitionSpec as P

GRID = 64
BLOCK = 256
LANE_BLOCK = 128
COORD_STEPS = 16


full_turn = 6.283185307179586
step_size = 0.5
smooth_weight = 0.5


def extended(cells, sides, width):
    for axis, dim in sides:
        count = lax.axis_size(axis)
        ends = count - 1
        head = lax.slice_in_dim(cells, 0, width, axis=dim)
        tail = lax.slice_in_dim(cells, cells.shape[dim] - width, cells.shape[dim], axis=dim)
        cells = jnp.concatenate(
            [
                lax.ppermute(tail, axis, [(i, (i + 1) % count) for i in range(ends)]),
                cells,
                lax.ppermute(head, axis, [((i + 1) % count, i) for i in range(ends)]),
            ],
            axis=dim,
        )
    return cells


def receiver_lookup_dict(table_row, antenna_ids):
    numbers = jnp.arange(table_row.shape[0], dtype=jnp.int32)
    return jnp.sum(
        jnp.where(antenna_ids[:, None] == numbers[None, :], table_row[None, :], 0.0), axis=1
    )


def turns(coord, pixel, image):
    whole = jnp.round(coord * COORD_STEPS).astype(jnp.int32)
    rest = coord - whole.astype(jnp.float32) / COORD_STEPS
    period = COORD_STEPS * image
    exact = jnp.bitwise_and(whole[None, :] * pixel, period - 1).astype(jnp.float32) / period
    return exact + rest[None, :] * pixel.astype(jnp.float32) / image


def phase_table(coord, starts, span, image):
    faces, chunks = starts.shape
    coarse = full_turn * turns(coord, starts.reshape(-1, 1), image)
    fine = full_turn * turns(coord, jnp.arange(span, dtype=jnp.int32)[:, None], image)
    coarse_c, coarse_s, fine_c, fine_s = lax.optimization_barrier(
        (jnp.cos(coarse), jnp.sin(coarse), jnp.cos(fine), jnp.sin(fine))
    )
    count = coord.shape[0]

    def spread(a):
        return jnp.broadcast_to(
            a.reshape(faces, chunks, 1, count), (faces, chunks, span, count)
        ).reshape(faces, chunks * span, count)

    def tile(a):
        return jnp.broadcast_to(a[None, None], (faces, chunks, span, count)).reshape(
            faces, chunks * span, count
        )

    pc, ps, qc, qs = spread(coarse_c), spread(coarse_s), tile(fine_c), tile(fine_s)
    return (pc * qc - ps * qs, ps * qc + pc * qs)


def exchange(x, n_vis, mask):
    return lax.ppermute(x, "vis", [(i, i ^ mask) for i in range(n_vis)])


def gather_rows(block, n_vis, tied):
    half = n_vis // 2
    me = lax.axis_index("vis")
    other = exchange(block, n_vis, half)
    other, tied = lax.optimization_barrier((other, tied))
    pair = jnp.where(me < half, jnp.stack([block, other]), jnp.stack([other, block]))
    groups = [list(range(half)), list(range(half, n_vis))]
    full = lax.all_to_all(
        jnp.broadcast_to(pair[None], (half,) + pair.shape), "vis", 0, 0, axis_index_groups=groups
    )
    return full.reshape((n_vis * block.shape[0],) + block.shape[1:]), tied


def reduce_rows(partial, n_vis, rows):
    half = n_vis // 2
    me = lax.axis_index("vis")
    slabs = partial.astype(jnp.bfloat16).reshape((half, 2, rows) + partial.shape[1:])
    groups = [list(range(half)), list(range(half, n_vis))]
    got = lax.all_to_all(slabs, "vis", 0, 0, axis_index_groups=groups)
    acc = jnp.sum(got.astype(jnp.float32), axis=0)
    mine = jnp.where(me < half, acc[0], acc[1])
    send = jnp.where(me < half, acc[1], acc[0]).astype(jnp.bfloat16)
    return mine + exchange(send, n_vis, half).astype(jnp.float32)


def local(
    patch_intensity,
    recorded_samples,
    sample_importance,
    block_populations,
    receiver_pairs,
    sample_rotation_phase,
    spectral_scaling,
    receiver_positions,
    patch_layout_position,
):
    rows_dev = patch_intensity.shape[0]
    ch_local = patch_intensity.shape[1]
    facets_here = patch_intensity.shape[2]
    facet = patch_intensity.shape[3]
    nvis = sample_importance.shape[0]
    n_vis = lax.axis_size("vis")
    image = GRID * facet
    norm_pred = 1.0 / math.sqrt(facets_here * facet * facet)
    norm_grad = 1.0 / math.sqrt(nvis * n_vis)
    sky_half = patch_intensity.astype(jnp.bfloat16)
    piece, (receiver_pairs, sample_rotation_phase) = gather_rows(
        sky_half, n_vis, (receiver_pairs, sample_rotation_phase)
    )
    eastward_shift = receiver_lookup_dict(
        receiver_positions[0], receiver_pairs[:, 0]
    ) - receiver_lookup_dict(receiver_positions[0], receiver_pairs[:, 1])
    northward_shift = receiver_lookup_dict(
        receiver_positions[1], receiver_pairs[:, 0]
    ) - receiver_lookup_dict(receiver_positions[1], receiver_pairs[:, 1])
    base_u = eastward_shift * jnp.cos(sample_rotation_phase) - northward_shift * jnp.sin(
        sample_rotation_phase
    )
    base_v = eastward_shift * jnp.sin(sample_rotation_phase) + northward_shift * jnp.cos(
        sample_rotation_phase
    )
    slots = jnp.arange(nvis, dtype=jnp.int32)
    block_of = slots // BLOCK
    block_numbers = jnp.arange(block_populations.shape[0], dtype=jnp.int32)
    block_count = jnp.sum(
        jnp.where(block_of[:, None] == block_numbers[None, :], block_populations[None, :], 0),
        axis=1,
    )
    scale_vis = (slots % BLOCK < block_count).astype(jnp.float32) * sample_importance
    first_row = patch_layout_position[:, 0] * facet - image // 2
    first_col = patch_layout_position[:, 1] * facet - image // 2
    chunk = jnp.arange(n_vis, dtype=jnp.int32)
    owner = (chunk % 2) * (n_vis // 2) + chunk // 2
    row_starts = first_row[:, None] + rows_dev * owner[None, :]
    col_starts = first_col[:, None] + LANE_BLOCK * jnp.arange(facet // LANE_BLOCK, dtype=jnp.int32)


    new_rows = []
    residuals = []
    for c in range(ch_local):
        coord_u = spectral_scaling[c] * base_u
        coord_v = spectral_scaling[c] * base_v
        row_cos, row_sin = phase_table(coord_u, row_starts, rows_dev, image)
        col_cos, col_sin = phase_table(coord_v, col_starts, LANE_BLOCK, image)
        cols = lax.optimization_barrier(
            jnp.concatenate([col_cos, col_sin], axis=2).astype(jnp.bfloat16)
        )
        sky_rows = jnp.transpose(piece[:, c], (1, 0, 2))
        waves = jnp.einsum("fij,fjk->fik", sky_rows, cols, preferred_element_type=jnp.float32)
        wave_c = waves[:, :, :nvis]
        wave_s = waves[:, :, nvis:]
        sum_re = jnp.sum(row_cos * wave_c - row_sin * wave_s, axis=(0, 1))
        sum_im = -jnp.sum(row_cos * wave_s + row_sin * wave_c, axis=(0, 1))
        resid_real = scale_vis * (norm_pred * sum_re - recorded_samples[c, 0])
        resid_imag = scale_vis * (norm_pred * sum_im - recorded_samples[c, 1])
        z_one = (row_cos * resid_real[None, None, :] - row_sin * resid_imag[None, None, :]).astype(
            jnp.bfloat16
        )
        z_two = (row_sin * resid_real[None, None, :] + row_cos * resid_imag[None, None, :]).astype(
            jnp.bfloat16
        )
        zs = jnp.concatenate([z_one, -z_two], axis=2)
        grad = jnp.einsum("fik,fjk->ifj", zs, cols, preferred_element_type=jnp.float32)
        new_rows.append(grad)
        residuals.append(jnp.stack([resid_real, resid_imag], axis=0))
    partial = jnp.stack(new_rows, axis=1)
    gradient = reduce_rows(partial, n_vis, rows_dev)
    padded = extended(patch_intensity.astype(jnp.bfloat16), (("chan", 1),), 1).astype(
        patch_intensity.dtype
    )
    left_side = padded[:, :-2]
    right_side = padded[:, 2:]
    chan_index = lax.axis_index("chan") * ch_local + jnp.arange(ch_local, dtype=jnp.int32)
    total_chan = ch_local * lax.axis_size("chan")
    has_left = (chan_index >= 1).astype(jnp.float32)[None, :, None, None]
    has_right = (chan_index <= total_chan - 2).astype(jnp.float32)[None, :, None, None]
    smooth = has_left * (patch_intensity - left_side) + has_right * (patch_intensity - right_side)
    new_sky = patch_intensity - step_size * (norm_grad * gradient + smooth_weight * smooth)
    residual = jnp.stack(residuals, axis=0)
    return (new_sky, residual)


def solution(mesh):
    return jax.shard_map(
        local,
        mesh=mesh,
        in_specs=(
            P("vis", "chan", None, None),
            P("chan", None, "vis"),
            P("vis"),
            P("vis"),
            P("vis", None),
            P("vis"),
            P("chan"),
            P(),
            P(),
        ),
        out_specs=(P("vis", "chan", None, None), P("chan", None, "vis")),
        check_vma=False,
    )
```

```python
import math

import jax
import jax.numpy as jnp
from jax import lax
from jax.experimental import pallas as pl
from jax.sharding import PartitionSpec as P

GRID = 64
BLOCK = 256
LANE_BLOCK = 128
COORD_STEPS = 16


full_turn = 6.283185307179586
step_size = 0.5
smooth_weight = 0.5


def extended(cells, sides, width):
    for axis, dim in sides:
        count = lax.axis_size(axis)
        ends = count - 1
        head = lax.slice_in_dim(cells, 0, width, axis=dim)
        tail = lax.slice_in_dim(cells, cells.shape[dim] - width, cells.shape[dim], axis=dim)
        cells = jnp.concatenate(
            [
                lax.ppermute(tail, axis, [(i, (i + 1) % count) for i in range(ends)]),
                cells,
                lax.ppermute(head, axis, [((i + 1) % count, i) for i in range(ends)]),
            ],
            axis=dim,
        )
    return cells


def receiver_lookup_dict(table_row, antenna_ids):
    numbers = jnp.arange(table_row.shape[0], dtype=jnp.int32)
    return jnp.sum(
        jnp.where(antenna_ids[:, None] == numbers[None, :], table_row[None, :], 0.0), axis=1
    )


def turns(coord, pixel, image):
    whole = jnp.round(coord * COORD_STEPS).astype(jnp.int32)
    rest = coord - whole.astype(jnp.float32) / COORD_STEPS
    period = COORD_STEPS * image
    exact = jnp.bitwise_and(whole[None, :] * pixel, period - 1).astype(jnp.float32) / period
    return exact + rest[None, :] * pixel.astype(jnp.float32) / image


def phase_factors(coord, starts, span, image):
    faces, chunks = starts.shape
    coarse = full_turn * turns(coord, starts.reshape(-1, 1), image)
    fine = full_turn * turns(coord, jnp.arange(span, dtype=jnp.int32)[:, None], image)
    coarse_c, coarse_s, fine_c, fine_s = lax.optimization_barrier(
        (jnp.cos(coarse), jnp.sin(coarse), jnp.cos(fine), jnp.sin(fine))
    )
    count = coord.shape[0]
    return (
        coarse_c.reshape(faces, chunks, count),
        coarse_s.reshape(faces, chunks, count),
        fine_c,
        fine_s,
    )


def phase_table(factors):
    coarse_c, coarse_s, fine_c, fine_s = factors
    faces, chunks, count = coarse_c.shape
    span = fine_c.shape[0]

    def spread(a):
        return jnp.broadcast_to(a[:, :, None, :], (faces, chunks, span, count)).reshape(
            faces, chunks * span, count
        )

    def tile(a):
        return jnp.broadcast_to(a[None, None], (faces, chunks, span, count)).reshape(
            faces, chunks * span, count
        )

    pc, ps, qc, qs = spread(coarse_c), spread(coarse_s), tile(fine_c), tile(fine_s)
    return (pc * qc - ps * qs, ps * qc + pc * qs)


def predict_kernel(sky_ref, ccos_ref, csin_ref, pc_ref, ps_ref, qc_ref, qs_ref, re_ref, im_ref):
    sky = sky_ref[...]
    wave_c = jnp.dot(sky, ccos_ref[...], preferred_element_type=jnp.float32)
    wave_s = jnp.dot(sky, csin_ref[...], preferred_element_type=jnp.float32)
    chunks = pc_ref.shape[0]
    span = qc_ref.shape[0]
    tk = wave_c.shape[1]
    wave_c = wave_c.reshape(chunks, span, tk)
    wave_s = wave_s.reshape(chunks, span, tk)
    qc = qc_ref[...][None]
    qs = qs_ref[...][None]
    a = jnp.sum(qc * wave_c - qs * wave_s, axis=1)
    b = jnp.sum(qs * wave_c + qc * wave_s, axis=1)
    pc = pc_ref[...]
    ps = ps_ref[...]
    re_ref[...] = jnp.sum(pc * a - ps * b, axis=0, keepdims=True)
    im_ref[...] = -jnp.sum(pc * b + ps * a, axis=0, keepdims=True)


def predict_sums(sky_rows, cols, factors, tk):
    coarse_c, coarse_s, fine_c, fine_s = factors
    faces, rows, width = sky_rows.shape
    chunks = coarse_c.shape[1]
    span = fine_c.shape[0]
    count = fine_c.shape[1]
    tiles = count // tk
    out = jax.ShapeDtypeStruct((faces, 1, count), jnp.float32)
    re, im = pl.pallas_call(
        predict_kernel,
        grid=(faces, tiles),
        in_specs=[
            pl.BlockSpec((None, rows, width), lambda f, t: (f, 0, 0)),
            pl.BlockSpec((None, width, tk), lambda f, t: (f, 0, t)),
            pl.BlockSpec((None, width, tk), lambda f, t: (f, 0, t + tiles)),
            pl.BlockSpec((None, chunks, tk), lambda f, t: (f, 0, t)),
            pl.BlockSpec((None, chunks, tk), lambda f, t: (f, 0, t)),
            pl.BlockSpec((span, tk), lambda f, t: (0, t)),
            pl.BlockSpec((span, tk), lambda f, t: (0, t)),
        ],
        out_specs=[
            pl.BlockSpec((None, 1, tk), lambda f, t: (f, 0, t)),
            pl.BlockSpec((None, 1, tk), lambda f, t: (f, 0, t)),
        ],
        out_shape=[out, out],
    )(sky_rows, cols, cols, coarse_c, coarse_s, fine_c, fine_s)
    return jnp.sum(re, axis=(0, 1)), jnp.sum(im, axis=(0, 1))


def exchange(x, n_vis, mask):
    return lax.ppermute(x, "vis", [(i, i ^ mask) for i in range(n_vis)])


def gather_rows(block, n_vis, tied):
    half = n_vis // 2
    me = lax.axis_index("vis")
    other = exchange(block, n_vis, half)
    other, tied = lax.optimization_barrier((other, tied))
    pair = jnp.where(me < half, jnp.stack([block, other]), jnp.stack([other, block]))
    groups = [list(range(half)), list(range(half, n_vis))]
    full = lax.all_to_all(
        jnp.broadcast_to(pair[None], (half,) + pair.shape), "vis", 0, 0, axis_index_groups=groups
    )
    return full.reshape((n_vis * block.shape[0],) + block.shape[1:]), tied


def reduce_rows(partial, n_vis, rows):
    half = n_vis // 2
    me = lax.axis_index("vis")
    slabs = partial.astype(jnp.bfloat16).reshape((half, 2, rows) + partial.shape[1:])
    groups = [list(range(half)), list(range(half, n_vis))]
    got = lax.all_to_all(slabs, "vis", 0, 0, axis_index_groups=groups)
    acc = jnp.sum(got.astype(jnp.float32), axis=0)
    mine = jnp.where(me < half, acc[0], acc[1])
    send = jnp.where(me < half, acc[1], acc[0]).astype(jnp.bfloat16)
    return mine + exchange(send, n_vis, half).astype(jnp.float32)


def local(
    patch_intensity,
    recorded_samples,
    sample_importance,
    block_populations,
    receiver_pairs,
    sample_rotation_phase,
    spectral_scaling,
    receiver_positions,
    patch_layout_position,
):
    rows_dev = patch_intensity.shape[0]
    ch_local = patch_intensity.shape[1]
    facets_here = patch_intensity.shape[2]
    facet = patch_intensity.shape[3]
    nvis = sample_importance.shape[0]
    n_vis = lax.axis_size("vis")
    image = GRID * facet
    norm_pred = 1.0 / math.sqrt(facets_here * facet * facet)
    norm_grad = 1.0 / math.sqrt(nvis * n_vis)
    sky_half = patch_intensity.astype(jnp.bfloat16)
    piece, (receiver_pairs, sample_rotation_phase) = gather_rows(
        sky_half, n_vis, (receiver_pairs, sample_rotation_phase)
    )
    eastward_shift = receiver_lookup_dict(
        receiver_positions[0], receiver_pairs[:, 0]
    ) - receiver_lookup_dict(receiver_positions[0], receiver_pairs[:, 1])
    northward_shift = receiver_lookup_dict(
        receiver_positions[1], receiver_pairs[:, 0]
    ) - receiver_lookup_dict(receiver_positions[1], receiver_pairs[:, 1])
    base_u = eastward_shift * jnp.cos(sample_rotation_phase) - northward_shift * jnp.sin(
        sample_rotation_phase
    )
    base_v = eastward_shift * jnp.sin(sample_rotation_phase) + northward_shift * jnp.cos(
        sample_rotation_phase
    )
    slots = jnp.arange(nvis, dtype=jnp.int32)
    block_of = slots // BLOCK
    block_numbers = jnp.arange(block_populations.shape[0], dtype=jnp.int32)
    block_count = jnp.sum(
        jnp.where(block_of[:, None] == block_numbers[None, :], block_populations[None, :], 0),
        axis=1,
    )
    scale_vis = (slots % BLOCK < block_count).astype(jnp.float32) * sample_importance
    first_row = patch_layout_position[:, 0] * facet - image // 2
    first_col = patch_layout_position[:, 1] * facet - image // 2
    chunk = jnp.arange(n_vis, dtype=jnp.int32)
    owner = (chunk % 2) * (n_vis // 2) + chunk // 2
    row_starts = first_row[:, None] + rows_dev * owner[None, :]
    col_starts = first_col[:, None] + LANE_BLOCK * jnp.arange(facet // LANE_BLOCK, dtype=jnp.int32)


    new_rows = []
    residuals = []
    for c in range(ch_local):
        coord_u = spectral_scaling[c] * base_u
        coord_v = spectral_scaling[c] * base_v
        row_factors = phase_factors(coord_u, row_starts, rows_dev, image)
        row_cos, row_sin = phase_table(row_factors)
        col_cos, col_sin = phase_table(phase_factors(coord_v, col_starts, LANE_BLOCK, image))
        cols = lax.optimization_barrier(
            jnp.concatenate([col_cos, col_sin], axis=2).astype(jnp.bfloat16)
        )
        sky_rows = jnp.transpose(piece[:, c], (1, 0, 2))
        sum_re, sum_im = predict_sums(sky_rows, cols, row_factors, min(nvis, 512))
        resid_real = scale_vis * (norm_pred * sum_re - recorded_samples[c, 0])
        resid_imag = scale_vis * (norm_pred * sum_im - recorded_samples[c, 1])
        z_one = (row_cos * resid_real[None, None, :] - row_sin * resid_imag[None, None, :]).astype(
            jnp.bfloat16
        )
        z_two = (row_sin * resid_real[None, None, :] + row_cos * resid_imag[None, None, :]).astype(
            jnp.bfloat16
        )
        zs = jnp.concatenate([z_one, -z_two], axis=2)
        grad = jnp.einsum("fik,fjk->ifj", zs, cols, preferred_element_type=jnp.float32)
        new_rows.append(grad)
        residuals.append(jnp.stack([resid_real, resid_imag], axis=0))
    partial = jnp.stack(new_rows, axis=1)
    gradient = reduce_rows(partial, n_vis, rows_dev)
    padded = extended(patch_intensity.astype(jnp.bfloat16), (("chan", 1),), 1).astype(
        patch_intensity.dtype
    )
    left_side = padded[:, :-2]
    right_side = padded[:, 2:]
    chan_index = lax.axis_index("chan") * ch_local + jnp.arange(ch_local, dtype=jnp.int32)
    total_chan = ch_local * lax.axis_size("chan")
    has_left = (chan_index >= 1).astype(jnp.float32)[None, :, None, None]
    has_right = (chan_index <= total_chan - 2).astype(jnp.float32)[None, :, None, None]
    smooth = has_left * (patch_intensity - left_side) + has_right * (patch_intensity - right_side)
    new_sky = patch_intensity - step_size * (norm_grad * gradient + smooth_weight * smooth)
    residual = jnp.stack(residuals, axis=0)
    return (new_sky, residual)


def solution(mesh):
    return jax.shard_map(
        local,
        mesh=mesh,
        in_specs=(
            P("vis", "chan", None, None),
            P("chan", None, "vis"),
            P("vis"),
            P("vis"),
            P("vis", None),
            P("vis"),
            P("chan"),
            P(),
            P(),
        ),
        out_specs=(P("vis", "chan", None, None), P("chan", None, "vis")),
        check_vma=False,
    )
```

```python
import math

import jax
import jax.numpy as jnp
from jax import lax
from jax.sharding import PartitionSpec as P

GRID = 64
BLOCK = 256
LANE_BLOCK = 128
COORD_STEPS = 16


full_turn = 6.283185307179586
step_size = 0.5
smooth_weight = 0.5


def extended(cells, sides, width):
    for axis, dim in sides:
        count = lax.axis_size(axis)
        ends = count - 1
        head = lax.slice_in_dim(cells, 0, width, axis=dim)
        tail = lax.slice_in_dim(cells, cells.shape[dim] - width, cells.shape[dim], axis=dim)
        cells = jnp.concatenate(
            [
                lax.ppermute(tail, axis, [(i, (i + 1) % count) for i in range(ends)]),
                cells,
                lax.ppermute(head, axis, [((i + 1) % count, i) for i in range(ends)]),
            ],
            axis=dim,
        )
    return cells


def receiver_lookup_dict(table_row, antenna_ids):
    numbers = jnp.arange(table_row.shape[0], dtype=jnp.int32)
    return jnp.sum(
        jnp.where(antenna_ids[:, None] == numbers[None, :], table_row[None, :], 0.0), axis=1
    )


def turns(coord, pixel, image):
    whole = jnp.round(coord * COORD_STEPS).astype(jnp.int32)
    rest = coord - whole.astype(jnp.float32) / COORD_STEPS
    period = COORD_STEPS * image
    exact = jnp.bitwise_and(whole[None, :] * pixel, period - 1).astype(jnp.float32) / period
    return exact + rest[None, :] * pixel.astype(jnp.float32) / image


def phase_factors(coord, starts, span, image):
    faces, chunks = starts.shape
    coarse = full_turn * turns(coord, starts.reshape(-1, 1), image)
    fine = full_turn * turns(coord, jnp.arange(span, dtype=jnp.int32)[:, None], image)
    coarse_c, coarse_s, fine_c, fine_s = lax.optimization_barrier(
        (jnp.cos(coarse), jnp.sin(coarse), jnp.cos(fine), jnp.sin(fine))
    )
    count = coord.shape[0]
    return (
        coarse_c.reshape(faces, chunks, count),
        coarse_s.reshape(faces, chunks, count),
        fine_c,
        fine_s,
    )


def spread(a, span):
    faces, chunks, count = a.shape
    return jnp.broadcast_to(a[:, :, None, :], (faces, chunks, span, count)).reshape(
        faces, chunks * span, count
    )


def tile(a, faces, chunks):
    span, count = a.shape
    return jnp.broadcast_to(a[None, None], (faces, chunks, span, count)).reshape(
        faces, chunks * span, count
    )


def rotate(factors, fine_c, fine_s):
    coarse_c, coarse_s = factors[0], factors[1]
    faces, chunks, _ = coarse_c.shape
    span = fine_c.shape[0]
    pc, ps = spread(coarse_c, span), spread(coarse_s, span)
    qc, qs = tile(fine_c, faces, chunks), tile(fine_s, faces, chunks)
    return (pc * qc - ps * qs, ps * qc + pc * qs)


def phase_table(factors):
    return rotate(factors, factors[2], factors[3])


def exchange(x, n_vis, mask):
    return lax.ppermute(x, "vis", [(i, i ^ mask) for i in range(n_vis)])


def gather_rows(block, n_vis, tied):
    half = n_vis // 2
    me = lax.axis_index("vis")
    other = exchange(block, n_vis, half)
    other, tied = lax.optimization_barrier((other, tied))
    pair = jnp.where(me < half, jnp.stack([block, other]), jnp.stack([other, block]))
    groups = [list(range(half)), list(range(half, n_vis))]
    full = lax.all_to_all(
        jnp.broadcast_to(pair[None], (half,) + pair.shape), "vis", 0, 0, axis_index_groups=groups
    )
    return full.reshape((n_vis * block.shape[0],) + block.shape[1:]), tied


def reduce_rows(partial, n_vis, rows):
    half = n_vis // 2
    me = lax.axis_index("vis")
    slabs = partial.astype(jnp.bfloat16).reshape((half, 2, rows) + partial.shape[1:])
    groups = [list(range(half)), list(range(half, n_vis))]
    got = lax.all_to_all(slabs, "vis", 0, 0, axis_index_groups=groups)
    acc = jnp.sum(got.astype(jnp.float32), axis=0)
    mine = jnp.where(me < half, acc[0], acc[1])
    send = jnp.where(me < half, acc[1], acc[0]).astype(jnp.bfloat16)
    return mine + exchange(send, n_vis, half).astype(jnp.float32)


def local(
    patch_intensity,
    recorded_samples,
    sample_importance,
    block_populations,
    receiver_pairs,
    sample_rotation_phase,
    spectral_scaling,
    receiver_positions,
    patch_layout_position,
):
    rows_dev = patch_intensity.shape[0]
    ch_local = patch_intensity.shape[1]
    facets_here = patch_intensity.shape[2]
    facet = patch_intensity.shape[3]
    nvis = sample_importance.shape[0]
    n_vis = lax.axis_size("vis")
    image = GRID * facet
    norm_pred = 1.0 / math.sqrt(facets_here * facet * facet)
    norm_grad = 1.0 / math.sqrt(nvis * n_vis)
    sky_half = patch_intensity.astype(jnp.bfloat16)
    piece, (receiver_pairs, sample_rotation_phase) = gather_rows(
        sky_half, n_vis, (receiver_pairs, sample_rotation_phase)
    )
    eastward_shift = receiver_lookup_dict(
        receiver_positions[0], receiver_pairs[:, 0]
    ) - receiver_lookup_dict(receiver_positions[0], receiver_pairs[:, 1])
    northward_shift = receiver_lookup_dict(
        receiver_positions[1], receiver_pairs[:, 0]
    ) - receiver_lookup_dict(receiver_positions[1], receiver_pairs[:, 1])
    base_u = eastward_shift * jnp.cos(sample_rotation_phase) - northward_shift * jnp.sin(
        sample_rotation_phase
    )
    base_v = eastward_shift * jnp.sin(sample_rotation_phase) + northward_shift * jnp.cos(
        sample_rotation_phase
    )
    slots = jnp.arange(nvis, dtype=jnp.int32)
    block_of = slots // BLOCK
    block_numbers = jnp.arange(block_populations.shape[0], dtype=jnp.int32)
    block_count = jnp.sum(
        jnp.where(block_of[:, None] == block_numbers[None, :], block_populations[None, :], 0),
        axis=1,
    )
    scale_vis = (slots % BLOCK < block_count).astype(jnp.float32) * sample_importance
    first_row = patch_layout_position[:, 0] * facet - image // 2
    first_col = patch_layout_position[:, 1] * facet - image // 2
    chunk = jnp.arange(n_vis, dtype=jnp.int32)
    owner = (chunk % 2) * (n_vis // 2) + chunk // 2
    row_starts = first_row[:, None] + rows_dev * owner[None, :]
    col_starts = first_col[:, None] + LANE_BLOCK * jnp.arange(facet // LANE_BLOCK, dtype=jnp.int32)


    new_rows = []
    residuals = []
    for c in range(ch_local):
        coord_u = spectral_scaling[c] * base_u
        coord_v = spectral_scaling[c] * base_v
        row_factors = phase_factors(coord_u, row_starts, rows_dev, image)
        row_cos, row_sin = phase_table(row_factors)
        col_cos, col_sin = phase_table(phase_factors(coord_v, col_starts, LANE_BLOCK, image))
        cols = lax.optimization_barrier(
            jnp.concatenate([col_cos, col_sin], axis=2).astype(jnp.bfloat16)
        )
        sky_rows = jnp.transpose(piece[:, c], (1, 0, 2))
        waves = jnp.einsum("fij,fjk->fik", sky_rows, cols, preferred_element_type=jnp.float32)
        wave_c = waves[:, :, :nvis]
        wave_s = waves[:, :, nvis:]
        sum_re = jnp.sum(row_cos * wave_c - row_sin * wave_s, axis=(0, 1))
        sum_im = -jnp.sum(row_cos * wave_s + row_sin * wave_c, axis=(0, 1))
        resid_real = scale_vis * (norm_pred * sum_re - recorded_samples[c, 0])
        resid_imag = scale_vis * (norm_pred * sum_im - recorded_samples[c, 1])
        fine_c, fine_s = row_factors[2], row_factors[3]
        turned_c = fine_c * resid_real[None, :] - fine_s * resid_imag[None, :]
        turned_s = fine_s * resid_real[None, :] + fine_c * resid_imag[None, :]
        z_one, z_two = rotate(row_factors, turned_c, turned_s)
        z_one = z_one.astype(jnp.bfloat16)
        z_two = z_two.astype(jnp.bfloat16)
        zs = jnp.concatenate([z_one, -z_two], axis=2)
        grad = jnp.einsum("fik,fjk->ifj", zs, cols, preferred_element_type=jnp.float32)
        new_rows.append(grad)
        residuals.append(jnp.stack([resid_real, resid_imag], axis=0))
    partial = jnp.stack(new_rows, axis=1)
    gradient = reduce_rows(partial, n_vis, rows_dev)
    padded = extended(patch_intensity.astype(jnp.bfloat16), (("chan", 1),), 1).astype(
        patch_intensity.dtype
    )
    left_side = padded[:, :-2]
    right_side = padded[:, 2:]
    chan_index = lax.axis_index("chan") * ch_local + jnp.arange(ch_local, dtype=jnp.int32)
    total_chan = ch_local * lax.axis_size("chan")
    has_left = (chan_index >= 1).astype(jnp.float32)[None, :, None, None]
    has_right = (chan_index <= total_chan - 2).astype(jnp.float32)[None, :, None, None]
    smooth = has_left * (patch_intensity - left_side) + has_right * (patch_intensity - right_side)
    new_sky = patch_intensity - step_size * (norm_grad * gradient + smooth_weight * smooth)
    residual = jnp.stack(residuals, axis=0)
    return (new_sky, residual)


def solution(mesh):
    return jax.shard_map(
        local,
        mesh=mesh,
        in_specs=(
            P("vis", "chan", None, None),
            P("chan", None, "vis"),
            P("vis"),
            P("vis"),
            P("vis", None),
            P("vis"),
            P("chan"),
            P(),
            P(),
        ),
        out_specs=(P("vis", "chan", None, None), P("chan", None, "vis")),
        check_vma=False,
    )
```

```python
import math

import jax
import jax.numpy as jnp
from jax import lax
from jax.sharding import PartitionSpec as P

GRID = 64
BLOCK = 256
LANE_BLOCK = 128
COORD_STEPS = 16


full_turn = 6.283185307179586
step_size = 0.5
smooth_weight = 0.5


def extended(cells, sides, width):
    for axis, dim in sides:
        count = lax.axis_size(axis)
        ends = count - 1
        head = lax.slice_in_dim(cells, 0, width, axis=dim)
        tail = lax.slice_in_dim(cells, cells.shape[dim] - width, cells.shape[dim], axis=dim)
        cells = jnp.concatenate(
            [
                lax.ppermute(tail, axis, [(i, (i + 1) % count) for i in range(ends)]),
                cells,
                lax.ppermute(head, axis, [((i + 1) % count, i) for i in range(ends)]),
            ],
            axis=dim,
        )
    return cells


def receiver_lookup_dict(table_row, antenna_ids):
    numbers = jnp.arange(table_row.shape[0], dtype=jnp.int32)
    return jnp.sum(
        jnp.where(antenna_ids[:, None] == numbers[None, :], table_row[None, :], 0.0), axis=1
    )


def turns(coord, pixel, image):
    whole = jnp.round(coord * COORD_STEPS).astype(jnp.int32)
    rest = coord - whole.astype(jnp.float32) / COORD_STEPS
    period = COORD_STEPS * image
    exact = jnp.bitwise_and(whole[None, :] * pixel, period - 1).astype(jnp.float32) / period
    return exact + rest[None, :] * pixel.astype(jnp.float32) / image


def phase_factors(coord, starts, span, image):
    faces, chunks = starts.shape
    coarse = full_turn * turns(coord, starts.reshape(-1, 1), image)
    fine = full_turn * turns(coord, jnp.arange(span, dtype=jnp.int32)[:, None], image)
    coarse_c, coarse_s, fine_c, fine_s = lax.optimization_barrier(
        (jnp.cos(coarse), jnp.sin(coarse), jnp.cos(fine), jnp.sin(fine))
    )
    count = coord.shape[0]
    return (
        coarse_c.reshape(faces, chunks, count),
        coarse_s.reshape(faces, chunks, count),
        fine_c,
        fine_s,
    )


def spread(a, span):
    faces, chunks, count = a.shape
    return jnp.broadcast_to(a[:, :, None, :], (faces, chunks, span, count)).reshape(
        faces, chunks * span, count
    )


def tile(a, faces, chunks):
    span, count = a.shape
    return jnp.broadcast_to(a[None, None], (faces, chunks, span, count)).reshape(
        faces, chunks * span, count
    )


def rotate(factors, fine_c, fine_s):
    coarse_c, coarse_s = factors[0], factors[1]
    faces, chunks, _ = coarse_c.shape
    span = fine_c.shape[0]
    pc, ps = spread(coarse_c, span), spread(coarse_s, span)
    qc, qs = tile(fine_c, faces, chunks), tile(fine_s, faces, chunks)
    return (pc * qc - ps * qs, ps * qc + pc * qs)


def phase_table(factors):
    return rotate(factors, factors[2], factors[3])


def exchange(x, n_vis, mask):
    return lax.ppermute(x, "vis", [(i, i ^ mask) for i in range(n_vis)])


def gather_rows(block, n_vis, tied):
    half = n_vis // 2
    me = lax.axis_index("vis")
    other = exchange(block, n_vis, half)
    other, tied = lax.optimization_barrier((other, tied))
    pair = jnp.where(me < half, jnp.stack([block, other]), jnp.stack([other, block]))
    groups = [list(range(half)), list(range(half, n_vis))]
    full = lax.all_to_all(
        jnp.broadcast_to(pair[None], (half,) + pair.shape), "vis", 0, 0, axis_index_groups=groups
    )
    return full.reshape((n_vis * block.shape[0],) + block.shape[1:]), tied


def reduce_rows(partial, n_vis, rows):
    half = n_vis // 2
    me = lax.axis_index("vis")
    slabs = partial.astype(jnp.bfloat16).reshape((half, 2, rows) + partial.shape[1:])
    groups = [list(range(half)), list(range(half, n_vis))]
    got = lax.all_to_all(slabs, "vis", 0, 0, axis_index_groups=groups)
    acc = jnp.sum(got.astype(jnp.float32), axis=0)
    mine = jnp.where(me < half, acc[0], acc[1])
    send = jnp.where(me < half, acc[1], acc[0]).astype(jnp.bfloat16)
    return mine + exchange(send, n_vis, half).astype(jnp.float32)


def local(
    patch_intensity,
    recorded_samples,
    sample_importance,
    block_populations,
    receiver_pairs,
    sample_rotation_phase,
    spectral_scaling,
    receiver_positions,
    patch_layout_position,
):
    rows_dev = patch_intensity.shape[0]
    ch_local = patch_intensity.shape[1]
    facets_here = patch_intensity.shape[2]
    facet = patch_intensity.shape[3]
    nvis = sample_importance.shape[0]
    n_vis = lax.axis_size("vis")
    image = GRID * facet
    norm_pred = 1.0 / math.sqrt(facets_here * facet * facet)
    norm_grad = 1.0 / math.sqrt(nvis * n_vis)
    sky_half = patch_intensity.astype(jnp.bfloat16)
    piece, (receiver_pairs, sample_rotation_phase) = gather_rows(
        sky_half, n_vis, (receiver_pairs, sample_rotation_phase)
    )
    eastward_shift = receiver_lookup_dict(
        receiver_positions[0], receiver_pairs[:, 0]
    ) - receiver_lookup_dict(receiver_positions[0], receiver_pairs[:, 1])
    northward_shift = receiver_lookup_dict(
        receiver_positions[1], receiver_pairs[:, 0]
    ) - receiver_lookup_dict(receiver_positions[1], receiver_pairs[:, 1])
    base_u = eastward_shift * jnp.cos(sample_rotation_phase) - northward_shift * jnp.sin(
        sample_rotation_phase
    )
    base_v = eastward_shift * jnp.sin(sample_rotation_phase) + northward_shift * jnp.cos(
        sample_rotation_phase
    )
    slots = jnp.arange(nvis, dtype=jnp.int32)
    block_of = slots // BLOCK
    block_numbers = jnp.arange(block_populations.shape[0], dtype=jnp.int32)
    block_count = jnp.sum(
        jnp.where(block_of[:, None] == block_numbers[None, :], block_populations[None, :], 0),
        axis=1,
    )
    scale_vis = (slots % BLOCK < block_count).astype(jnp.float32) * sample_importance
    first_row = patch_layout_position[:, 0] * facet - image // 2
    first_col = patch_layout_position[:, 1] * facet - image // 2
    chunk = jnp.arange(n_vis, dtype=jnp.int32)
    owner = (chunk % 2) * (n_vis // 2) + chunk // 2
    row_starts = first_row[:, None] + rows_dev * owner[None, :]
    col_starts = first_col[:, None] + LANE_BLOCK * jnp.arange(facet // LANE_BLOCK, dtype=jnp.int32)


    new_rows = []
    residuals = []
    for c in range(ch_local):
        coord_u = spectral_scaling[c] * base_u
        coord_v = spectral_scaling[c] * base_v
        row_factors = phase_factors(coord_u, row_starts, rows_dev, image)
        row_cos, row_sin = phase_table(row_factors)
        col_cos, col_sin = phase_table(phase_factors(coord_v, col_starts, LANE_BLOCK, image))
        cols = jnp.concatenate([col_cos, col_sin], axis=2).astype(jnp.bfloat16)
        sky_rows = jnp.transpose(piece[:, c], (1, 0, 2))
        waves = jnp.einsum("fij,fjk->fik", sky_rows, cols, preferred_element_type=jnp.float32)
        wave_c = waves[:, :, :nvis]
        wave_s = waves[:, :, nvis:]
        sum_re = jnp.sum(row_cos * wave_c - row_sin * wave_s, axis=(0, 1))
        sum_im = -jnp.sum(row_cos * wave_s + row_sin * wave_c, axis=(0, 1))
        resid_real = scale_vis * (norm_pred * sum_re - recorded_samples[c, 0])
        resid_imag = scale_vis * (norm_pred * sum_im - recorded_samples[c, 1])
        fine_c, fine_s = row_factors[2], row_factors[3]
        turned_c = fine_c * resid_real[None, :] - fine_s * resid_imag[None, :]
        turned_s = fine_s * resid_real[None, :] + fine_c * resid_imag[None, :]
        z_one, z_two = rotate(row_factors, turned_c, turned_s)
        z_one = z_one.astype(jnp.bfloat16)
        z_two = z_two.astype(jnp.bfloat16)
        zs = jnp.concatenate([z_one, -z_two], axis=2)
        grad = jnp.einsum("fik,fjk->ifj", zs, cols, preferred_element_type=jnp.float32)
        new_rows.append(grad)
        residuals.append(jnp.stack([resid_real, resid_imag], axis=0))
    partial = jnp.stack(new_rows, axis=1)
    gradient = reduce_rows(partial, n_vis, rows_dev)
    padded = extended(patch_intensity.astype(jnp.bfloat16), (("chan", 1),), 1).astype(
        patch_intensity.dtype
    )
    left_side = padded[:, :-2]
    right_side = padded[:, 2:]
    chan_index = lax.axis_index("chan") * ch_local + jnp.arange(ch_local, dtype=jnp.int32)
    total_chan = ch_local * lax.axis_size("chan")
    has_left = (chan_index >= 1).astype(jnp.float32)[None, :, None, None]
    has_right = (chan_index <= total_chan - 2).astype(jnp.float32)[None, :, None, None]
    smooth = has_left * (patch_intensity - left_side) + has_right * (patch_intensity - right_side)
    new_sky = patch_intensity - step_size * (norm_grad * gradient + smooth_weight * smooth)
    residual = jnp.stack(residuals, axis=0)
    return (new_sky, residual)


def solution(mesh):
    return jax.shard_map(
        local,
        mesh=mesh,
        in_specs=(
            P("vis", "chan", None, None),
            P("chan", None, "vis"),
            P("vis"),
            P("vis"),
            P("vis", None),
            P("vis"),
            P("chan"),
            P(),
            P(),
        ),
        out_specs=(P("vis", "chan", None, None), P("chan", None, "vis")),
        check_vma=False,
    )
```

```python
import math

import jax
import jax.numpy as jnp
from jax import lax
from jax.sharding import PartitionSpec as P

GRID = 64
BLOCK = 256
LANE_BLOCK = 128
COORD_STEPS = 16


full_turn = 6.283185307179586
step_size = 0.5
smooth_weight = 0.5


def extended(cells, sides, width):
    for axis, dim in sides:
        count = lax.axis_size(axis)
        ends = count - 1
        head = lax.slice_in_dim(cells, 0, width, axis=dim)
        tail = lax.slice_in_dim(cells, cells.shape[dim] - width, cells.shape[dim], axis=dim)
        cells = jnp.concatenate(
            [
                lax.ppermute(tail, axis, [(i, (i + 1) % count) for i in range(ends)]),
                cells,
                lax.ppermute(head, axis, [((i + 1) % count, i) for i in range(ends)]),
            ],
            axis=dim,
        )
    return cells


def receiver_lookup_dict(table_row, antenna_ids):
    numbers = jnp.arange(table_row.shape[0], dtype=jnp.int32)
    return jnp.sum(
        jnp.where(antenna_ids[:, None] == numbers[None, :], table_row[None, :], 0.0), axis=1
    )


def turns(coord, pixel, image):
    whole = jnp.round(coord * COORD_STEPS).astype(jnp.int32)
    rest = coord - whole.astype(jnp.float32) / COORD_STEPS
    period = COORD_STEPS * image
    exact = jnp.bitwise_and(whole[None, :] * pixel, period - 1).astype(jnp.float32) / period
    return exact + rest[None, :] * pixel.astype(jnp.float32) / image


def phase_factors(coord, starts, span, image):
    faces, chunks = starts.shape
    coarse = full_turn * turns(coord, starts.reshape(-1, 1), image)
    fine = full_turn * turns(coord, jnp.arange(span, dtype=jnp.int32)[:, None], image)
    coarse_c, coarse_s, fine_c, fine_s = lax.optimization_barrier(
        (jnp.cos(coarse), jnp.sin(coarse), jnp.cos(fine), jnp.sin(fine))
    )
    count = coord.shape[0]
    return (
        coarse_c.reshape(faces, chunks, count),
        coarse_s.reshape(faces, chunks, count),
        fine_c,
        fine_s,
    )


def spread(a, span):
    faces, chunks, count = a.shape
    return jnp.broadcast_to(a[:, :, None, :], (faces, chunks, span, count)).reshape(
        faces, chunks * span, count
    )


def tile(a, faces, chunks):
    span, count = a.shape
    return jnp.broadcast_to(a[None, None], (faces, chunks, span, count)).reshape(
        faces, chunks * span, count
    )


def rotate(factors, fine_c, fine_s):
    coarse_c, coarse_s = factors[0], factors[1]
    faces, chunks, _ = coarse_c.shape
    span = fine_c.shape[0]
    pc, ps = spread(coarse_c, span), spread(coarse_s, span)
    qc, qs = tile(fine_c, faces, chunks), tile(fine_s, faces, chunks)
    return (pc * qc - ps * qs, ps * qc + pc * qs)


def phase_table(factors):
    return rotate(factors, factors[2], factors[3])


def exchange(x, n_vis, mask):
    return lax.ppermute(x, "vis", [(i, i ^ mask) for i in range(n_vis)])


def gather_rows(block, n_vis, tied):
    half = n_vis // 2
    me = lax.axis_index("vis")
    other = exchange(block, n_vis, half)
    other, tied = lax.optimization_barrier((other, tied))
    wide = (half, 2) + block.shape
    mine = jnp.broadcast_to(block[None, None], wide)
    theirs = jnp.broadcast_to(other[None, None], wide)
    slot = lax.broadcasted_iota(jnp.int32, wide, 1)
    groups = [list(range(half)), list(range(half, n_vis))]
    full = lax.all_to_all(
        jnp.where((slot == 0) == (me < half), mine, theirs), "vis", 0, 0, axis_index_groups=groups
    )
    return full.reshape((n_vis * block.shape[0],) + block.shape[1:]), tied


def reduce_rows(partial, n_vis, rows):
    half = n_vis // 2
    me = lax.axis_index("vis")
    slabs = partial.astype(jnp.bfloat16).reshape((half, 2, rows) + partial.shape[1:])
    groups = [list(range(half)), list(range(half, n_vis))]
    got = lax.all_to_all(slabs, "vis", 0, 0, axis_index_groups=groups)
    acc = jnp.sum(got.astype(jnp.float32), axis=0)
    mine = jnp.where(me < half, acc[0], acc[1])
    send = jnp.where(me < half, acc[1], acc[0]).astype(jnp.bfloat16)
    return mine + exchange(send, n_vis, half).astype(jnp.float32)


def local(
    patch_intensity,
    recorded_samples,
    sample_importance,
    block_populations,
    receiver_pairs,
    sample_rotation_phase,
    spectral_scaling,
    receiver_positions,
    patch_layout_position,
):
    rows_dev = patch_intensity.shape[0]
    ch_local = patch_intensity.shape[1]
    facets_here = patch_intensity.shape[2]
    facet = patch_intensity.shape[3]
    nvis = sample_importance.shape[0]
    n_vis = lax.axis_size("vis")
    image = GRID * facet
    norm_pred = 1.0 / math.sqrt(facets_here * facet * facet)
    norm_grad = 1.0 / math.sqrt(nvis * n_vis)
    sky_half = patch_intensity.astype(jnp.bfloat16)
    piece, (receiver_pairs, sample_rotation_phase) = gather_rows(
        sky_half, n_vis, (receiver_pairs, sample_rotation_phase)
    )
    eastward_shift = receiver_lookup_dict(
        receiver_positions[0], receiver_pairs[:, 0]
    ) - receiver_lookup_dict(receiver_positions[0], receiver_pairs[:, 1])
    northward_shift = receiver_lookup_dict(
        receiver_positions[1], receiver_pairs[:, 0]
    ) - receiver_lookup_dict(receiver_positions[1], receiver_pairs[:, 1])
    base_u = eastward_shift * jnp.cos(sample_rotation_phase) - northward_shift * jnp.sin(
        sample_rotation_phase
    )
    base_v = eastward_shift * jnp.sin(sample_rotation_phase) + northward_shift * jnp.cos(
        sample_rotation_phase
    )
    slots = jnp.arange(nvis, dtype=jnp.int32)
    block_of = slots // BLOCK
    block_numbers = jnp.arange(block_populations.shape[0], dtype=jnp.int32)
    block_count = jnp.sum(
        jnp.where(block_of[:, None] == block_numbers[None, :], block_populations[None, :], 0),
        axis=1,
    )
    scale_vis = (slots % BLOCK < block_count).astype(jnp.float32) * sample_importance
    first_row = patch_layout_position[:, 0] * facet - image // 2
    first_col = patch_layout_position[:, 1] * facet - image // 2
    chunk = jnp.arange(n_vis, dtype=jnp.int32)
    owner = (chunk % 2) * (n_vis // 2) + chunk // 2
    row_starts = first_row[:, None] + rows_dev * owner[None, :]
    col_starts = first_col[:, None] + LANE_BLOCK * jnp.arange(facet // LANE_BLOCK, dtype=jnp.int32)


    new_rows = []
    residuals = []
    for c in range(ch_local):
        coord_u = spectral_scaling[c] * base_u
        coord_v = spectral_scaling[c] * base_v
        row_factors = phase_factors(coord_u, row_starts, rows_dev, image)
        row_cos, row_sin = phase_table(row_factors)
        col_cos, col_sin = phase_table(phase_factors(coord_v, col_starts, LANE_BLOCK, image))
        cols = jnp.concatenate([col_cos, col_sin], axis=2).astype(jnp.bfloat16)
        sky_rows = jnp.transpose(piece[:, c], (1, 0, 2))
        waves = jnp.einsum("fij,fjk->fik", sky_rows, cols, preferred_element_type=jnp.float32)
        wave_c = waves[:, :, :nvis]
        wave_s = waves[:, :, nvis:]
        sum_re = jnp.sum(row_cos * wave_c - row_sin * wave_s, axis=(0, 1))
        sum_im = -jnp.sum(row_cos * wave_s + row_sin * wave_c, axis=(0, 1))
        resid_real = scale_vis * (norm_pred * sum_re - recorded_samples[c, 0])
        resid_imag = scale_vis * (norm_pred * sum_im - recorded_samples[c, 1])
        fine_c, fine_s = row_factors[2], row_factors[3]
        turned_c = fine_c * resid_real[None, :] - fine_s * resid_imag[None, :]
        turned_s = fine_s * resid_real[None, :] + fine_c * resid_imag[None, :]
        z_one, z_two = rotate(row_factors, turned_c, turned_s)
        z_one = z_one.astype(jnp.bfloat16)
        z_two = z_two.astype(jnp.bfloat16)
        zs = jnp.concatenate([z_one, -z_two], axis=2)
        grad = jnp.einsum("fik,fjk->ifj", zs, cols, preferred_element_type=jnp.float32)
        new_rows.append(grad)
        residuals.append(jnp.stack([resid_real, resid_imag], axis=0))
    partial = jnp.stack(new_rows, axis=1)
    gradient = reduce_rows(partial, n_vis, rows_dev)
    padded = extended(patch_intensity.astype(jnp.bfloat16), (("chan", 1),), 1).astype(
        patch_intensity.dtype
    )
    left_side = padded[:, :-2]
    right_side = padded[:, 2:]
    chan_index = lax.axis_index("chan") * ch_local + jnp.arange(ch_local, dtype=jnp.int32)
    total_chan = ch_local * lax.axis_size("chan")
    has_left = (chan_index >= 1).astype(jnp.float32)[None, :, None, None]
    has_right = (chan_index <= total_chan - 2).astype(jnp.float32)[None, :, None, None]
    smooth = has_left * (patch_intensity - left_side) + has_right * (patch_intensity - right_side)
    new_sky = patch_intensity - step_size * (norm_grad * gradient + smooth_weight * smooth)
    residual = jnp.stack(residuals, axis=0)
    return (new_sky, residual)


def solution(mesh):
    return jax.shard_map(
        local,
        mesh=mesh,
        in_specs=(
            P("vis", "chan", None, None),
            P("chan", None, "vis"),
            P("vis"),
            P("vis"),
            P("vis", None),
            P("vis"),
            P("chan"),
            P(),
            P(),
        ),
        out_specs=(P("vis", "chan", None, None), P("chan", None, "vis")),
        check_vma=False,
    )
```

```python
import math

import jax
import jax.numpy as jnp
from jax import lax
from jax.sharding import PartitionSpec as P

GRID = 64
BLOCK = 256
LANE_BLOCK = 128
COORD_STEPS = 16


full_turn = 6.283185307179586
step_size = 0.5
smooth_weight = 0.5


def extended(cells, sides, width):
    for axis, dim in sides:
        count = lax.axis_size(axis)
        ends = count - 1
        head = lax.slice_in_dim(cells, 0, width, axis=dim)
        tail = lax.slice_in_dim(cells, cells.shape[dim] - width, cells.shape[dim], axis=dim)
        cells = jnp.concatenate(
            [
                lax.ppermute(tail, axis, [(i, (i + 1) % count) for i in range(ends)]),
                cells,
                lax.ppermute(head, axis, [((i + 1) % count, i) for i in range(ends)]),
            ],
            axis=dim,
        )
    return cells


def receiver_lookup_dict(table_row, antenna_ids):
    numbers = jnp.arange(table_row.shape[0], dtype=jnp.int32)
    return jnp.sum(
        jnp.where(antenna_ids[:, None] == numbers[None, :], table_row[None, :], 0.0), axis=1
    )


def turns(coord, pixel, image):
    whole = jnp.round(coord * COORD_STEPS).astype(jnp.int32)
    rest = coord - whole.astype(jnp.float32) / COORD_STEPS
    period = COORD_STEPS * image
    exact = jnp.bitwise_and(whole[None, :] * pixel, period - 1).astype(jnp.float32) / period
    return exact + rest[None, :] * pixel.astype(jnp.float32) / image


def phase_factors(coord, starts, span, image):
    faces, chunks = starts.shape
    coarse = full_turn * turns(coord, starts.reshape(-1, 1), image)
    fine = full_turn * turns(coord, jnp.arange(span, dtype=jnp.int32)[:, None], image)
    coarse_c, coarse_s, fine_c, fine_s = lax.optimization_barrier(
        (jnp.cos(coarse), jnp.sin(coarse), jnp.cos(fine), jnp.sin(fine))
    )
    count = coord.shape[0]
    return (
        coarse_c.reshape(faces, chunks, count),
        coarse_s.reshape(faces, chunks, count),
        fine_c,
        fine_s,
    )


def spread(a, span):
    faces, chunks, count = a.shape
    return jnp.broadcast_to(a[:, :, None, :], (faces, chunks, span, count)).reshape(
        faces, chunks * span, count
    )


def tile(a, faces, chunks):
    span, count = a.shape
    return jnp.broadcast_to(a[None, None], (faces, chunks, span, count)).reshape(
        faces, chunks * span, count
    )


def rotate(factors, fine_c, fine_s):
    coarse_c, coarse_s = factors[0], factors[1]
    faces, chunks, _ = coarse_c.shape
    span = fine_c.shape[0]
    pc, ps = spread(coarse_c, span), spread(coarse_s, span)
    qc, qs = tile(fine_c, faces, chunks), tile(fine_s, faces, chunks)
    return (pc * qc - ps * qs, ps * qc + pc * qs)


def phase_table(factors):
    return rotate(factors, factors[2], factors[3])


def exchange(x, n_vis, mask):
    return lax.ppermute(x, "vis", [(i, i ^ mask) for i in range(n_vis)])


def gather_rows(block, n_vis, tied):
    half = n_vis // 2
    me = lax.axis_index("vis")
    other = exchange(block, n_vis, half)
    other, tied = lax.optimization_barrier((other, tied))
    wide = (half, 2) + block.shape
    mine = jnp.broadcast_to(block[None, None], wide)
    theirs = jnp.broadcast_to(other[None, None], wide)
    slot = lax.broadcasted_iota(jnp.int32, wide, 1)
    groups = [list(range(half)), list(range(half, n_vis))]
    full = lax.all_to_all(
        jnp.where((slot == 0) == (me < half), mine, theirs), "vis", 0, 0, axis_index_groups=groups
    )
    return full.reshape((n_vis * block.shape[0],) + block.shape[1:]), tied


def reduce_rows(partial, n_vis, rows):
    half = n_vis // 2
    me = lax.axis_index("vis")
    slabs = partial.astype(jnp.bfloat16).reshape((half, 2, rows) + partial.shape[1:])
    groups = [list(range(half)), list(range(half, n_vis))]
    got = lax.all_to_all(slabs, "vis", 0, 0, axis_index_groups=groups)
    acc = jnp.sum(got.astype(jnp.float32), axis=0)
    mine = jnp.where(me < half, acc[0], acc[1])
    send = jnp.where(me < half, acc[1], acc[0]).astype(jnp.bfloat16)
    return mine + exchange(send, n_vis, half).astype(jnp.float32)


def local(
    patch_intensity,
    recorded_samples,
    sample_importance,
    block_populations,
    receiver_pairs,
    sample_rotation_phase,
    spectral_scaling,
    receiver_positions,
    patch_layout_position,
):
    rows_dev = patch_intensity.shape[0]
    ch_local = patch_intensity.shape[1]
    facets_here = patch_intensity.shape[2]
    facet = patch_intensity.shape[3]
    nvis = sample_importance.shape[0]
    n_vis = lax.axis_size("vis")
    image = GRID * facet
    norm_pred = 1.0 / math.sqrt(facets_here * facet * facet)
    norm_grad = 1.0 / math.sqrt(nvis * n_vis)
    sky_half = lax.optimization_barrier(patch_intensity.astype(jnp.bfloat16))
    piece, (receiver_pairs, sample_rotation_phase) = gather_rows(
        sky_half, n_vis, (receiver_pairs, sample_rotation_phase)
    )
    eastward_shift = receiver_lookup_dict(
        receiver_positions[0], receiver_pairs[:, 0]
    ) - receiver_lookup_dict(receiver_positions[0], receiver_pairs[:, 1])
    northward_shift = receiver_lookup_dict(
        receiver_positions[1], receiver_pairs[:, 0]
    ) - receiver_lookup_dict(receiver_positions[1], receiver_pairs[:, 1])
    base_u = eastward_shift * jnp.cos(sample_rotation_phase) - northward_shift * jnp.sin(
        sample_rotation_phase
    )
    base_v = eastward_shift * jnp.sin(sample_rotation_phase) + northward_shift * jnp.cos(
        sample_rotation_phase
    )
    slots = jnp.arange(nvis, dtype=jnp.int32)
    block_of = slots // BLOCK
    block_numbers = jnp.arange(block_populations.shape[0], dtype=jnp.int32)
    block_count = jnp.sum(
        jnp.where(block_of[:, None] == block_numbers[None, :], block_populations[None, :], 0),
        axis=1,
    )
    scale_vis = (slots % BLOCK < block_count).astype(jnp.float32) * sample_importance
    first_row = patch_layout_position[:, 0] * facet - image // 2
    first_col = patch_layout_position[:, 1] * facet - image // 2
    chunk = jnp.arange(n_vis, dtype=jnp.int32)
    owner = (chunk % 2) * (n_vis // 2) + chunk // 2
    row_starts = first_row[:, None] + rows_dev * owner[None, :]
    col_starts = first_col[:, None] + LANE_BLOCK * jnp.arange(facet // LANE_BLOCK, dtype=jnp.int32)


    new_rows = []
    residuals = []
    for c in range(ch_local):
        coord_u = spectral_scaling[c] * base_u
        coord_v = spectral_scaling[c] * base_v
        row_factors = phase_factors(coord_u, row_starts, rows_dev, image)
        row_cos, row_sin = phase_table(row_factors)
        col_cos, col_sin = phase_table(phase_factors(coord_v, col_starts, LANE_BLOCK, image))
        cols = jnp.concatenate([col_cos, col_sin], axis=2).astype(jnp.bfloat16)
        sky_rows = jnp.transpose(piece[:, c], (1, 0, 2))
        waves = jnp.einsum("fij,fjk->fik", sky_rows, cols, preferred_element_type=jnp.float32)
        wave_c = waves[:, :, :nvis]
        wave_s = waves[:, :, nvis:]
        sum_re = jnp.sum(row_cos * wave_c - row_sin * wave_s, axis=(0, 1))
        sum_im = -jnp.sum(row_cos * wave_s + row_sin * wave_c, axis=(0, 1))
        resid_real = scale_vis * (norm_pred * sum_re - recorded_samples[c, 0])
        resid_imag = scale_vis * (norm_pred * sum_im - recorded_samples[c, 1])
        fine_c, fine_s = row_factors[2], row_factors[3]
        turned_c = fine_c * resid_real[None, :] - fine_s * resid_imag[None, :]
        turned_s = fine_s * resid_real[None, :] + fine_c * resid_imag[None, :]
        z_one, z_two = rotate(row_factors, turned_c, turned_s)
        z_one = z_one.astype(jnp.bfloat16)
        z_two = z_two.astype(jnp.bfloat16)
        zs = jnp.concatenate([z_one, -z_two], axis=2)
        grad = jnp.einsum("fik,fjk->ifj", zs, cols, preferred_element_type=jnp.float32)
        new_rows.append(grad)
        residuals.append(jnp.stack([resid_real, resid_imag], axis=0))
    partial = jnp.stack(new_rows, axis=1)
    gradient = reduce_rows(partial, n_vis, rows_dev)
    padded = extended(sky_half, (("chan", 1),), 1).astype(
        patch_intensity.dtype
    )
    left_side = padded[:, :-2]
    right_side = padded[:, 2:]
    chan_index = lax.axis_index("chan") * ch_local + jnp.arange(ch_local, dtype=jnp.int32)
    total_chan = ch_local * lax.axis_size("chan")
    has_left = (chan_index >= 1).astype(jnp.float32)[None, :, None, None]
    has_right = (chan_index <= total_chan - 2).astype(jnp.float32)[None, :, None, None]
    smooth = has_left * (patch_intensity - left_side) + has_right * (patch_intensity - right_side)
    new_sky = patch_intensity - step_size * (norm_grad * gradient + smooth_weight * smooth)
    residual = jnp.stack(residuals, axis=0)
    return (new_sky, residual)


def solution(mesh):
    return jax.shard_map(
        local,
        mesh=mesh,
        in_specs=(
            P("vis", "chan", None, None),
            P("chan", None, "vis"),
            P("vis"),
            P("vis"),
            P("vis", None),
            P("vis"),
            P("chan"),
            P(),
            P(),
        ),
        out_specs=(P("vis", "chan", None, None), P("chan", None, "vis")),
        check_vma=False,
    )
```

```python
import math

import jax
import jax.numpy as jnp
import numpy as np
from jax import lax
from jax.sharding import PartitionSpec as P

GRID = 64
BLOCK = 256
LANE_BLOCK = 128
COORD_STEPS = 16


full_turn = 6.283185307179586
step_size = 0.5
smooth_weight = 0.5


def extended(cells, sides, width):
    for axis, dim in sides:
        count = lax.axis_size(axis)
        ends = count - 1
        head = lax.slice_in_dim(cells, 0, width, axis=dim)
        tail = lax.slice_in_dim(cells, cells.shape[dim] - width, cells.shape[dim], axis=dim)
        cells = jnp.concatenate(
            [
                lax.ppermute(tail, axis, [(i, (i + 1) % count) for i in range(ends)]),
                cells,
                lax.ppermute(head, axis, [((i + 1) % count, i) for i in range(ends)]),
            ],
            axis=dim,
        )
    return cells


def receiver_lookup_dict(table_row, antenna_ids):
    numbers = jnp.arange(table_row.shape[0], dtype=jnp.int32)
    return jnp.sum(
        jnp.where(antenna_ids[:, None] == numbers[None, :], table_row[None, :], 0.0), axis=1
    )


def turns(coord, pixel, image):
    whole = jnp.round(coord * COORD_STEPS).astype(jnp.int32)
    rest = coord - whole.astype(jnp.float32) / COORD_STEPS
    period = COORD_STEPS * image
    exact = jnp.bitwise_and(whole[None, :] * pixel, period - 1).astype(jnp.float32) / period
    return exact + rest[None, :] * pixel.astype(jnp.float32) / image


def phase_factors(coord, starts, span, image):
    faces, chunks = starts.shape
    coarse = full_turn * turns(coord, starts.reshape(-1, 1), image)
    fine = full_turn * turns(coord, jnp.arange(span, dtype=jnp.int32)[:, None], image)
    coarse_c, coarse_s, fine_c, fine_s = lax.optimization_barrier(
        (jnp.cos(coarse), jnp.sin(coarse), jnp.cos(fine), jnp.sin(fine))
    )
    count = coord.shape[0]
    return (
        coarse_c.reshape(faces, chunks, count),
        coarse_s.reshape(faces, chunks, count),
        fine_c,
        fine_s,
    )


def spread(a, span):
    faces, chunks, count = a.shape
    return jnp.broadcast_to(a[:, :, None, :], (faces, chunks, span, count)).reshape(
        faces, chunks * span, count
    )


def tile(a, faces, chunks):
    span, count = a.shape
    return jnp.broadcast_to(a[None, None], (faces, chunks, span, count)).reshape(
        faces, chunks * span, count
    )


def rotate(factors, fine_c, fine_s):
    coarse_c, coarse_s = factors[0], factors[1]
    faces, chunks, _ = coarse_c.shape
    span = fine_c.shape[0]
    pc, ps = spread(coarse_c, span), spread(coarse_s, span)
    qc, qs = tile(fine_c, faces, chunks), tile(fine_s, faces, chunks)
    return (pc * qc - ps * qs, ps * qc + pc * qs)


def phase_table(factors):
    return rotate(factors, factors[2], factors[3])


def exchange(x, n_vis, mask):
    return lax.ppermute(x, "vis", [(i, i ^ mask) for i in range(n_vis)])


def gather_rows(block, n_vis, tied):
    half = n_vis // 2
    me = lax.axis_index("vis")
    other = exchange(block, n_vis, half)
    other, tied = lax.optimization_barrier((other, tied))
    wide = (half, 2) + block.shape
    mine = jnp.broadcast_to(block[None, None], wide)
    theirs = jnp.broadcast_to(other[None, None], wide)
    slot = lax.broadcasted_iota(jnp.int32, wide, 1)
    groups = [list(range(half)), list(range(half, n_vis))]
    full = lax.all_to_all(
        jnp.where((slot == 0) == (me < half), mine, theirs), "vis", 0, 0, axis_index_groups=groups
    )
    return full.reshape((n_vis * block.shape[0],) + block.shape[1:]), tied


def reduce_rows(partial, n_vis, rows):
    half = n_vis // 2
    me = lax.axis_index("vis")
    slabs = partial.astype(jnp.bfloat16).reshape((half, 2, rows) + partial.shape[1:])
    groups = [list(range(half)), list(range(half, n_vis))]
    got = lax.all_to_all(slabs, "vis", 0, 0, axis_index_groups=groups)
    acc = jnp.sum(got.astype(jnp.float32), axis=0)
    mine = jnp.where(me < half, acc[0], acc[1])
    send = jnp.where(me < half, acc[1], acc[0]).astype(jnp.bfloat16)
    return mine + exchange(send, n_vis, half).astype(jnp.float32)


def local(
    patch_intensity,
    recorded_samples,
    sample_importance,
    block_populations,
    receiver_pairs,
    sample_rotation_phase,
    spectral_scaling,
    receiver_positions,
    patch_layout_position,
):
    rows_dev = patch_intensity.shape[0]
    ch_local = patch_intensity.shape[1]
    facets_here = patch_intensity.shape[2]
    facet = patch_intensity.shape[3]
    nvis = sample_importance.shape[0]
    n_vis = lax.axis_size("vis")
    image = GRID * facet
    norm_pred = 1.0 / math.sqrt(facets_here * facet * facet)
    norm_grad = 1.0 / math.sqrt(nvis * n_vis)
    sky_half = lax.optimization_barrier(patch_intensity.astype(jnp.bfloat16))
    piece, (receiver_pairs, sample_rotation_phase) = gather_rows(
        sky_half, n_vis, (receiver_pairs, sample_rotation_phase)
    )
    eastward_shift = receiver_lookup_dict(
        receiver_positions[0], receiver_pairs[:, 0]
    ) - receiver_lookup_dict(receiver_positions[0], receiver_pairs[:, 1])
    northward_shift = receiver_lookup_dict(
        receiver_positions[1], receiver_pairs[:, 0]
    ) - receiver_lookup_dict(receiver_positions[1], receiver_pairs[:, 1])
    base_u = eastward_shift * jnp.cos(sample_rotation_phase) - northward_shift * jnp.sin(
        sample_rotation_phase
    )
    base_v = eastward_shift * jnp.sin(sample_rotation_phase) + northward_shift * jnp.cos(
        sample_rotation_phase
    )
    slots = jnp.arange(nvis, dtype=jnp.int32)
    block_count = jnp.broadcast_to(
        block_populations[:, None], (block_populations.shape[0], BLOCK)
    ).reshape(nvis)
    scale_vis = (slots % BLOCK < block_count).astype(jnp.float32) * sample_importance
    first_row = patch_layout_position[:, 0] * facet - image // 2
    first_col = patch_layout_position[:, 1] * facet - image // 2
    chunk = np.arange(n_vis, dtype=np.int32)
    owner = (chunk % 2) * (n_vis // 2) + chunk // 2
    row_starts = first_row[:, None] + jnp.asarray(rows_dev * owner, jnp.int32)[None, :]
    col_offsets = LANE_BLOCK * np.arange(facet // LANE_BLOCK, dtype=np.int32)
    col_starts = first_col[:, None] + jnp.asarray(col_offsets, jnp.int32)[None, :]


    new_rows = []
    residuals = []
    for c in range(ch_local):
        coord_u = spectral_scaling[c] * base_u
        coord_v = spectral_scaling[c] * base_v
        row_factors = phase_factors(coord_u, row_starts, rows_dev, image)
        row_cos, row_sin = phase_table(row_factors)
        col_cos, col_sin = phase_table(phase_factors(coord_v, col_starts, LANE_BLOCK, image))
        cols = jnp.concatenate([col_cos, col_sin], axis=2).astype(jnp.bfloat16)
        sky_rows = jnp.transpose(piece[:, c], (1, 0, 2))
        waves = jnp.einsum("fij,fjk->fik", sky_rows, cols, preferred_element_type=jnp.float32)
        wave_c = waves[:, :, :nvis]
        wave_s = waves[:, :, nvis:]
        sum_re = jnp.sum(row_cos * wave_c - row_sin * wave_s, axis=(0, 1))
        sum_im = -jnp.sum(row_cos * wave_s + row_sin * wave_c, axis=(0, 1))
        resid_real = scale_vis * (norm_pred * sum_re - recorded_samples[c, 0])
        resid_imag = scale_vis * (norm_pred * sum_im - recorded_samples[c, 1])
        fine_c, fine_s = row_factors[2], row_factors[3]
        turned_c = fine_c * resid_real[None, :] - fine_s * resid_imag[None, :]
        turned_s = fine_s * resid_real[None, :] + fine_c * resid_imag[None, :]
        z_one, z_two = rotate(row_factors, turned_c, turned_s)
        z_one = z_one.astype(jnp.bfloat16)
        z_two = z_two.astype(jnp.bfloat16)
        zs = jnp.concatenate([z_one, -z_two], axis=2)
        grad = jnp.einsum("fik,fjk->ifj", zs, cols, preferred_element_type=jnp.float32)
        new_rows.append(grad)
        residuals.append(jnp.stack([resid_real, resid_imag], axis=0))
    partial = jnp.stack(new_rows, axis=1)
    gradient = reduce_rows(partial, n_vis, rows_dev)
    padded = extended(sky_half, (("chan", 1),), 1).astype(
        patch_intensity.dtype
    )
    left_side = padded[:, :-2]
    right_side = padded[:, 2:]
    chan_index = lax.axis_index("chan") * ch_local + jnp.arange(ch_local, dtype=jnp.int32)
    total_chan = ch_local * lax.axis_size("chan")
    has_left = (chan_index >= 1).astype(jnp.float32)[None, :, None, None]
    has_right = (chan_index <= total_chan - 2).astype(jnp.float32)[None, :, None, None]
    smooth = has_left * (patch_intensity - left_side) + has_right * (patch_intensity - right_side)
    new_sky = patch_intensity - step_size * (norm_grad * gradient + smooth_weight * smooth)
    residual = jnp.stack(residuals, axis=0)
    return (new_sky, residual)


def solution(mesh):
    return jax.shard_map(
        local,
        mesh=mesh,
        in_specs=(
            P("vis", "chan", None, None),
            P("chan", None, "vis"),
            P("vis"),
            P("vis"),
            P("vis", None),
            P("vis"),
            P("chan"),
            P(),
            P(),
        ),
        out_specs=(P("vis", "chan", None, None), P("chan", None, "vis")),
        check_vma=False,
    )
```

```python
import math

import jax
import jax.numpy as jnp
import numpy as np
from jax import lax
from jax.sharding import PartitionSpec as P

GRID = 64
BLOCK = 256
LANE_BLOCK = 128
COORD_STEPS = 16


full_turn = 6.283185307179586
step_size = 0.5
smooth_weight = 0.5


def extended(cells, sides, width):
    for axis, dim in sides:
        count = lax.axis_size(axis)
        ends = count - 1
        head = lax.slice_in_dim(cells, 0, width, axis=dim)
        tail = lax.slice_in_dim(cells, cells.shape[dim] - width, cells.shape[dim], axis=dim)
        cells = jnp.concatenate(
            [
                lax.ppermute(tail, axis, [(i, (i + 1) % count) for i in range(ends)]),
                cells,
                lax.ppermute(head, axis, [((i + 1) % count, i) for i in range(ends)]),
            ],
            axis=dim,
        )
    return cells


def receiver_lookup_dict(table_row, antenna_ids):
    numbers = jnp.arange(table_row.shape[0], dtype=jnp.int32)
    return jnp.sum(
        jnp.where(antenna_ids[:, None] == numbers[None, :], table_row[None, :], 0.0), axis=1
    )


def turns(coord, pixel, image):
    whole = jnp.round(coord * COORD_STEPS).astype(jnp.int32)
    rest = coord - whole.astype(jnp.float32) / COORD_STEPS
    period = COORD_STEPS * image
    exact = jnp.bitwise_and(whole[None, :] * pixel, period - 1).astype(jnp.float32) / period
    return exact + rest[None, :] * pixel.astype(jnp.float32) / image


def phase_factors(coord, starts, span, image):
    faces, chunks = starts.shape
    coarse = full_turn * turns(coord, starts.reshape(-1, 1), image)
    fine = full_turn * turns(coord, jnp.arange(span, dtype=jnp.int32)[:, None], image)
    coarse_c, coarse_s, fine_c, fine_s = lax.optimization_barrier(
        (jnp.cos(coarse), jnp.sin(coarse), jnp.cos(fine), jnp.sin(fine))
    )
    count = coord.shape[0]
    return (
        coarse_c.reshape(faces, chunks, count),
        coarse_s.reshape(faces, chunks, count),
        fine_c,
        fine_s,
    )


def spread(a, span):
    faces, chunks, count = a.shape
    return jnp.broadcast_to(a[:, :, None, :], (faces, chunks, span, count)).reshape(
        faces, chunks * span, count
    )


def tile(a, faces, chunks):
    span, count = a.shape
    return jnp.broadcast_to(a[None, None], (faces, chunks, span, count)).reshape(
        faces, chunks * span, count
    )


def rotate(factors, fine_c, fine_s):
    coarse_c, coarse_s = factors[0], factors[1]
    faces, chunks, _ = coarse_c.shape
    span = fine_c.shape[0]
    pc, ps = spread(coarse_c, span), spread(coarse_s, span)
    qc, qs = tile(fine_c, faces, chunks), tile(fine_s, faces, chunks)
    return (pc * qc - ps * qs, ps * qc + pc * qs)


def phase_table(factors):
    return rotate(factors, factors[2], factors[3])


def exchange(x, n_vis, mask):
    return lax.ppermute(x, "vis", [(i, i ^ mask) for i in range(n_vis)])


def gather_rows(block, n_vis, tied):
    half = n_vis // 2
    me = lax.axis_index("vis")
    other = exchange(block, n_vis, half)
    other, tied = lax.optimization_barrier((other, tied))
    wide = (half, 2) + block.shape
    mine = jnp.broadcast_to(block[None, None], wide)
    theirs = jnp.broadcast_to(other[None, None], wide)
    slot = lax.broadcasted_iota(jnp.int32, wide, 1)
    groups = [list(range(half)), list(range(half, n_vis))]
    full = lax.all_to_all(
        jnp.where((slot == 0) == (me < half), mine, theirs), "vis", 0, 0, axis_index_groups=groups
    )
    return full.reshape((n_vis * block.shape[0],) + block.shape[1:]), tied


def reduce_rows(partial, n_vis, rows):
    half = n_vis // 2
    me = lax.axis_index("vis")
    slabs = partial.astype(jnp.bfloat16).reshape((half, 2, rows) + partial.shape[1:])
    groups = [list(range(half)), list(range(half, n_vis))]
    got = lax.all_to_all(slabs, "vis", 0, 0, axis_index_groups=groups)
    acc = jnp.sum(got.astype(jnp.float32), axis=0)
    mine = jnp.where(me < half, acc[0], acc[1])
    send = jnp.where(me < half, acc[1], acc[0]).astype(jnp.bfloat16)
    return mine + exchange(send, n_vis, half).astype(jnp.float32)


def local(
    patch_intensity,
    recorded_samples,
    sample_importance,
    block_populations,
    receiver_pairs,
    sample_rotation_phase,
    spectral_scaling,
    receiver_positions,
    patch_layout_position,
):
    rows_dev = patch_intensity.shape[0]
    ch_local = patch_intensity.shape[1]
    facets_here = patch_intensity.shape[2]
    facet = patch_intensity.shape[3]
    nvis = sample_importance.shape[0]
    n_vis = lax.axis_size("vis")
    image = GRID * facet
    norm_pred = 1.0 / math.sqrt(facets_here * facet * facet)
    norm_grad = 1.0 / math.sqrt(nvis * n_vis)
    sky_half = lax.optimization_barrier(patch_intensity.astype(jnp.bfloat16))
    piece, (receiver_pairs, sample_rotation_phase) = gather_rows(
        sky_half, n_vis, (receiver_pairs, sample_rotation_phase)
    )
    eastward_shift = receiver_lookup_dict(
        receiver_positions[0], receiver_pairs[:, 0]
    ) - receiver_lookup_dict(receiver_positions[0], receiver_pairs[:, 1])
    northward_shift = receiver_lookup_dict(
        receiver_positions[1], receiver_pairs[:, 0]
    ) - receiver_lookup_dict(receiver_positions[1], receiver_pairs[:, 1])
    base_u = eastward_shift * jnp.cos(sample_rotation_phase) - northward_shift * jnp.sin(
        sample_rotation_phase
    )
    base_v = eastward_shift * jnp.sin(sample_rotation_phase) + northward_shift * jnp.cos(
        sample_rotation_phase
    )
    slots = jnp.arange(nvis, dtype=jnp.int32)
    block_count = jnp.broadcast_to(
        block_populations[:, None], (block_populations.shape[0], BLOCK)
    ).reshape(nvis)
    scale_vis = (slots % BLOCK < block_count).astype(jnp.float32) * sample_importance
    first_row = patch_layout_position[:, 0] * facet - image // 2
    first_col = patch_layout_position[:, 1] * facet - image // 2
    chunk = np.arange(n_vis, dtype=np.int32)
    owner = (chunk % 2) * (n_vis // 2) + chunk // 2
    row_starts = first_row[:, None] + jnp.asarray(rows_dev * owner, jnp.int32)[None, :]
    col_offsets = LANE_BLOCK * np.arange(facet // LANE_BLOCK, dtype=np.int32)
    col_starts = first_col[:, None] + jnp.asarray(col_offsets, jnp.int32)[None, :]


    new_rows = []
    residuals = []
    for c in range(ch_local):
        coord_u = spectral_scaling[c] * base_u
        coord_v = spectral_scaling[c] * base_v
        row_factors = phase_factors(coord_u, row_starts, rows_dev, image)
        col_cos, col_sin = phase_table(phase_factors(coord_v, col_starts, LANE_BLOCK, image))
        cols = jnp.concatenate([col_cos, col_sin], axis=2).astype(jnp.bfloat16)
        sky_rows = jnp.transpose(piece[:, c], (1, 0, 2))
        waves = jnp.einsum("fij,fjk->fik", sky_rows, cols, preferred_element_type=jnp.float32)
        wave_c = waves[:, :, :nvis]
        wave_s = waves[:, :, nvis:]
        coarse_c, coarse_s, fine_c, fine_s = row_factors
        faces, chunks, _ = coarse_c.shape
        wave_c = wave_c.reshape(faces, chunks, rows_dev, nvis)
        wave_s = wave_s.reshape(faces, chunks, rows_dev, nvis)
        part_a = jnp.sum(fine_c * wave_c - fine_s * wave_s, axis=2)
        part_b = jnp.sum(fine_s * wave_c + fine_c * wave_s, axis=2)
        sum_re = jnp.sum(coarse_c * part_a - coarse_s * part_b, axis=(0, 1))
        sum_im = -jnp.sum(coarse_c * part_b + coarse_s * part_a, axis=(0, 1))
        resid_real = scale_vis * (norm_pred * sum_re - recorded_samples[c, 0])
        resid_imag = scale_vis * (norm_pred * sum_im - recorded_samples[c, 1])
        fine_c, fine_s = row_factors[2], row_factors[3]
        turned_c = fine_c * resid_real[None, :] - fine_s * resid_imag[None, :]
        turned_s = fine_s * resid_real[None, :] + fine_c * resid_imag[None, :]
        z_one, z_two = rotate(row_factors, turned_c, turned_s)
        z_one = z_one.astype(jnp.bfloat16)
        z_two = z_two.astype(jnp.bfloat16)
        zs = jnp.concatenate([z_one, -z_two], axis=2)
        grad = jnp.einsum("fik,fjk->ifj", zs, cols, preferred_element_type=jnp.float32)
        new_rows.append(grad)
        residuals.append(jnp.stack([resid_real, resid_imag], axis=0))
    partial = jnp.stack(new_rows, axis=1)
    gradient = reduce_rows(partial, n_vis, rows_dev)
    padded = extended(sky_half, (("chan", 1),), 1).astype(
        patch_intensity.dtype
    )
    left_side = padded[:, :-2]
    right_side = padded[:, 2:]
    chan_index = lax.axis_index("chan") * ch_local + jnp.arange(ch_local, dtype=jnp.int32)
    total_chan = ch_local * lax.axis_size("chan")
    has_left = (chan_index >= 1).astype(jnp.float32)[None, :, None, None]
    has_right = (chan_index <= total_chan - 2).astype(jnp.float32)[None, :, None, None]
    smooth = has_left * (patch_intensity - left_side) + has_right * (patch_intensity - right_side)
    new_sky = patch_intensity - step_size * (norm_grad * gradient + smooth_weight * smooth)
    residual = jnp.stack(residuals, axis=0)
    return (new_sky, residual)


def solution(mesh):
    return jax.shard_map(
        local,
        mesh=mesh,
        in_specs=(
            P("vis", "chan", None, None),
            P("chan", None, "vis"),
            P("vis"),
            P("vis"),
            P("vis", None),
            P("vis"),
            P("chan"),
            P(),
            P(),
        ),
        out_specs=(P("vis", "chan", None, None), P("chan", None, "vis")),
        check_vma=False,
    )
```

```python
import math

import jax
import jax.numpy as jnp
import numpy as np
from jax import lax
from jax.experimental.layout import Layout, with_layout_constraint
from jax.sharding import PartitionSpec as P

GRID = 64
BLOCK = 256
LANE_BLOCK = 128
COORD_STEPS = 16


full_turn = 6.283185307179586
step_size = 0.5
smooth_weight = 0.5


def extended(cells, sides, width):
    for axis, dim in sides:
        count = lax.axis_size(axis)
        ends = count - 1
        head = lax.slice_in_dim(cells, 0, width, axis=dim)
        tail = lax.slice_in_dim(cells, cells.shape[dim] - width, cells.shape[dim], axis=dim)
        cells = jnp.concatenate(
            [
                lax.ppermute(tail, axis, [(i, (i + 1) % count) for i in range(ends)]),
                cells,
                lax.ppermute(head, axis, [((i + 1) % count, i) for i in range(ends)]),
            ],
            axis=dim,
        )
    return cells


def receiver_lookup_dict(table_row, antenna_ids):
    numbers = jnp.arange(table_row.shape[0], dtype=jnp.int32)
    return jnp.sum(
        jnp.where(antenna_ids[:, None] == numbers[None, :], table_row[None, :], 0.0), axis=1
    )


def turns(coord, pixel, image):
    whole = jnp.round(coord * COORD_STEPS).astype(jnp.int32)
    rest = coord - whole.astype(jnp.float32) / COORD_STEPS
    period = COORD_STEPS * image
    exact = jnp.bitwise_and(whole[None, :] * pixel, period - 1).astype(jnp.float32) / period
    return exact + rest[None, :] * pixel.astype(jnp.float32) / image


def phase_factors(coord, starts, span, image):
    faces, chunks = starts.shape
    coarse = full_turn * turns(coord, starts.reshape(-1, 1), image)
    fine = full_turn * turns(coord, jnp.arange(span, dtype=jnp.int32)[:, None], image)
    coarse_c, coarse_s, fine_c, fine_s = lax.optimization_barrier(
        (jnp.cos(coarse), jnp.sin(coarse), jnp.cos(fine), jnp.sin(fine))
    )
    count = coord.shape[0]
    return (
        coarse_c.reshape(faces, chunks, count),
        coarse_s.reshape(faces, chunks, count),
        fine_c,
        fine_s,
    )


def spread(a, span):
    faces, chunks, count = a.shape
    return jnp.broadcast_to(a[:, :, None, :], (faces, chunks, span, count)).reshape(
        faces, chunks * span, count
    )


def tile(a, faces, chunks):
    span, count = a.shape
    return jnp.broadcast_to(a[None, None], (faces, chunks, span, count)).reshape(
        faces, chunks * span, count
    )


def rotate(factors, fine_c, fine_s):
    coarse_c, coarse_s = factors[0], factors[1]
    faces, chunks, _ = coarse_c.shape
    span = fine_c.shape[0]
    pc, ps = spread(coarse_c, span), spread(coarse_s, span)
    qc, qs = tile(fine_c, faces, chunks), tile(fine_s, faces, chunks)
    return (pc * qc - ps * qs, ps * qc + pc * qs)


def phase_table(factors):
    return rotate(factors, factors[2], factors[3])


def exchange(x, n_vis, mask):
    return lax.ppermute(x, "vis", [(i, i ^ mask) for i in range(n_vis)])


def gather_rows(block, n_vis, tied):
    half = n_vis // 2
    me = lax.axis_index("vis")
    other = exchange(block, n_vis, half)
    other, tied = lax.optimization_barrier((other, tied))
    wide = (half, 2) + block.shape
    mine = jnp.broadcast_to(block[None, None], wide)
    theirs = jnp.broadcast_to(other[None, None], wide)
    slot = lax.broadcasted_iota(jnp.int32, wide, 1)
    groups = [list(range(half)), list(range(half, n_vis))]
    full = lax.all_to_all(
        jnp.where((slot == 0) == (me < half), mine, theirs), "vis", 0, 0, axis_index_groups=groups
    )
    return full.reshape((n_vis * block.shape[0],) + block.shape[1:]), tied


def reduce_rows(partial, n_vis, rows):
    half = n_vis // 2
    me = lax.axis_index("vis")
    slabs = partial.astype(jnp.bfloat16).reshape((half, 2, rows) + partial.shape[1:])
    slabs = with_layout_constraint(slabs, Layout(tuple(range(slabs.ndim)), None))
    groups = [list(range(half)), list(range(half, n_vis))]
    got = lax.all_to_all(slabs, "vis", 0, 0, axis_index_groups=groups)
    acc = jnp.sum(got.astype(jnp.float32), axis=0)
    mine = jnp.where(me < half, acc[0], acc[1])
    send = jnp.where(me < half, acc[1], acc[0]).astype(jnp.bfloat16)
    return mine + exchange(send, n_vis, half).astype(jnp.float32)


def local(
    patch_intensity,
    recorded_samples,
    sample_importance,
    block_populations,
    receiver_pairs,
    sample_rotation_phase,
    spectral_scaling,
    receiver_positions,
    patch_layout_position,
):
    rows_dev = patch_intensity.shape[0]
    ch_local = patch_intensity.shape[1]
    facets_here = patch_intensity.shape[2]
    facet = patch_intensity.shape[3]
    nvis = sample_importance.shape[0]
    n_vis = lax.axis_size("vis")
    image = GRID * facet
    norm_pred = 1.0 / math.sqrt(facets_here * facet * facet)
    norm_grad = 1.0 / math.sqrt(nvis * n_vis)
    sky_half = lax.optimization_barrier(patch_intensity.astype(jnp.bfloat16))
    piece, (receiver_pairs, sample_rotation_phase) = gather_rows(
        sky_half, n_vis, (receiver_pairs, sample_rotation_phase)
    )
    eastward_shift = receiver_lookup_dict(
        receiver_positions[0], receiver_pairs[:, 0]
    ) - receiver_lookup_dict(receiver_positions[0], receiver_pairs[:, 1])
    northward_shift = receiver_lookup_dict(
        receiver_positions[1], receiver_pairs[:, 0]
    ) - receiver_lookup_dict(receiver_positions[1], receiver_pairs[:, 1])
    base_u = eastward_shift * jnp.cos(sample_rotation_phase) - northward_shift * jnp.sin(
        sample_rotation_phase
    )
    base_v = eastward_shift * jnp.sin(sample_rotation_phase) + northward_shift * jnp.cos(
        sample_rotation_phase
    )
    slots = jnp.arange(nvis, dtype=jnp.int32)
    block_count = jnp.broadcast_to(
        block_populations[:, None], (block_populations.shape[0], BLOCK)
    ).reshape(nvis)
    scale_vis = (slots % BLOCK < block_count).astype(jnp.float32) * sample_importance
    first_row = patch_layout_position[:, 0] * facet - image // 2
    first_col = patch_layout_position[:, 1] * facet - image // 2
    chunk = np.arange(n_vis, dtype=np.int32)
    owner = (chunk % 2) * (n_vis // 2) + chunk // 2
    row_starts = first_row[:, None] + jnp.asarray(rows_dev * owner, jnp.int32)[None, :]
    col_offsets = LANE_BLOCK * np.arange(facet // LANE_BLOCK, dtype=np.int32)
    col_starts = first_col[:, None] + jnp.asarray(col_offsets, jnp.int32)[None, :]


    new_rows = []
    residuals = []
    for c in range(ch_local):
        coord_u = spectral_scaling[c] * base_u
        coord_v = spectral_scaling[c] * base_v
        row_factors = phase_factors(coord_u, row_starts, rows_dev, image)
        col_cos, col_sin = phase_table(phase_factors(coord_v, col_starts, LANE_BLOCK, image))
        cols = jnp.concatenate([col_cos, col_sin], axis=2).astype(jnp.bfloat16)
        sky_rows = jnp.transpose(piece[:, c], (1, 0, 2))
        waves = jnp.einsum("fij,fjk->fik", sky_rows, cols, preferred_element_type=jnp.float32)
        wave_c = waves[:, :, :nvis]
        wave_s = waves[:, :, nvis:]
        coarse_c, coarse_s, fine_c, fine_s = row_factors
        faces, chunks, _ = coarse_c.shape
        wave_c = wave_c.reshape(faces, chunks, rows_dev, nvis)
        wave_s = wave_s.reshape(faces, chunks, rows_dev, nvis)
        part_a = jnp.sum(fine_c * wave_c - fine_s * wave_s, axis=2)
        part_b = jnp.sum(fine_s * wave_c + fine_c * wave_s, axis=2)
        sum_re = jnp.sum(coarse_c * part_a - coarse_s * part_b, axis=(0, 1))
        sum_im = -jnp.sum(coarse_c * part_b + coarse_s * part_a, axis=(0, 1))
        resid_real = scale_vis * (norm_pred * sum_re - recorded_samples[c, 0])
        resid_imag = scale_vis * (norm_pred * sum_im - recorded_samples[c, 1])
        fine_c, fine_s = row_factors[2], row_factors[3]
        turned_c = fine_c * resid_real[None, :] - fine_s * resid_imag[None, :]
        turned_s = fine_s * resid_real[None, :] + fine_c * resid_imag[None, :]
        z_one, z_two = rotate(row_factors, turned_c, turned_s)
        z_one = z_one.astype(jnp.bfloat16)
        z_two = z_two.astype(jnp.bfloat16)
        zs = jnp.concatenate([z_one, -z_two], axis=2)
        grad = jnp.einsum("fik,fjk->ifj", zs, cols, preferred_element_type=jnp.float32)
        new_rows.append(grad)
        residuals.append(jnp.stack([resid_real, resid_imag], axis=0))
    partial = jnp.stack(new_rows, axis=1)
    gradient = reduce_rows(partial, n_vis, rows_dev)
    padded = extended(sky_half, (("chan", 1),), 1).astype(
        patch_intensity.dtype
    )
    left_side = padded[:, :-2]
    right_side = padded[:, 2:]
    chan_index = lax.axis_index("chan") * ch_local + jnp.arange(ch_local, dtype=jnp.int32)
    total_chan = ch_local * lax.axis_size("chan")
    has_left = (chan_index >= 1).astype(jnp.float32)[None, :, None, None]
    has_right = (chan_index <= total_chan - 2).astype(jnp.float32)[None, :, None, None]
    smooth = has_left * (patch_intensity - left_side) + has_right * (patch_intensity - right_side)
    new_sky = patch_intensity - step_size * (norm_grad * gradient + smooth_weight * smooth)
    residual = jnp.stack(residuals, axis=0)
    return (new_sky, residual)


def solution(mesh):
    return jax.shard_map(
        local,
        mesh=mesh,
        in_specs=(
            P("vis", "chan", None, None),
            P("chan", None, "vis"),
            P("vis"),
            P("vis"),
            P("vis", None),
            P("vis"),
            P("chan"),
            P(),
            P(),
        ),
        out_specs=(P("vis", "chan", None, None), P("chan", None, "vis")),
        check_vma=False,
    )
```

```python
import math

import jax
import jax.numpy as jnp
import numpy as np
from jax import lax
from jax.sharding import PartitionSpec as P

GRID = 64
BLOCK = 256
LANE_BLOCK = 128
COORD_STEPS = 16


full_turn = 6.283185307179586
step_size = 0.5
smooth_weight = 0.5


def extended(cells, sides, width):
    for axis, dim in sides:
        count = lax.axis_size(axis)
        ends = count - 1
        head = lax.slice_in_dim(cells, 0, width, axis=dim)
        tail = lax.slice_in_dim(cells, cells.shape[dim] - width, cells.shape[dim], axis=dim)
        cells = jnp.concatenate(
            [
                lax.ppermute(tail, axis, [(i, (i + 1) % count) for i in range(ends)]),
                cells,
                lax.ppermute(head, axis, [((i + 1) % count, i) for i in range(ends)]),
            ],
            axis=dim,
        )
    return cells


def receiver_lookup_dict(table_row, antenna_ids):
    numbers = jnp.arange(table_row.shape[0], dtype=jnp.int32)
    return jnp.sum(
        jnp.where(antenna_ids[:, None] == numbers[None, :], table_row[None, :], 0.0), axis=1
    )


def turns(coord, pixel, image):
    whole = jnp.round(coord * COORD_STEPS).astype(jnp.int32)
    rest = coord - whole.astype(jnp.float32) / COORD_STEPS
    period = COORD_STEPS * image
    exact = jnp.bitwise_and(whole[None, :] * pixel, period - 1).astype(jnp.float32) / period
    return exact + rest[None, :] * pixel.astype(jnp.float32) / image


def phase_factors(coord, starts, span, image):
    faces, chunks = starts.shape
    coarse = full_turn * turns(coord, starts.reshape(-1, 1), image)
    fine = full_turn * turns(coord, jnp.arange(span, dtype=jnp.int32)[:, None], image)
    coarse_c, coarse_s, fine_c, fine_s = lax.optimization_barrier(
        (jnp.cos(coarse), jnp.sin(coarse), jnp.cos(fine), jnp.sin(fine))
    )
    count = coord.shape[0]
    return (
        coarse_c.reshape(faces, chunks, count),
        coarse_s.reshape(faces, chunks, count),
        fine_c,
        fine_s,
    )


def spread(a, span):
    faces, chunks, count = a.shape
    return jnp.broadcast_to(a[:, :, None, :], (faces, chunks, span, count)).reshape(
        faces, chunks * span, count
    )


def tile(a, faces, chunks):
    span, count = a.shape
    return jnp.broadcast_to(a[None, None], (faces, chunks, span, count)).reshape(
        faces, chunks * span, count
    )


def rotate(factors, fine_c, fine_s):
    coarse_c, coarse_s = factors[0], factors[1]
    faces, chunks, _ = coarse_c.shape
    span = fine_c.shape[0]
    pc, ps = spread(coarse_c, span), spread(coarse_s, span)
    qc, qs = tile(fine_c, faces, chunks), tile(fine_s, faces, chunks)
    return (pc * qc - ps * qs, ps * qc + pc * qs)


def phase_table(factors):
    return rotate(factors, factors[2], factors[3])


def exchange(x, n_vis, mask):
    return lax.ppermute(x, "vis", [(i, i ^ mask) for i in range(n_vis)])


def gather_rows(block, n_vis, tied):
    half = n_vis // 2
    me = lax.axis_index("vis")
    other = exchange(block, n_vis, half)
    other, tied = lax.optimization_barrier((other, tied))
    wide = (half, 2) + block.shape
    mine = jnp.broadcast_to(block[None, None], wide)
    theirs = jnp.broadcast_to(other[None, None], wide)
    slot = lax.broadcasted_iota(jnp.int32, wide, 1)
    groups = [list(range(half)), list(range(half, n_vis))]
    full = lax.all_to_all(
        jnp.where((slot == 0) == (me < half), mine, theirs), "vis", 0, 0, axis_index_groups=groups
    )
    return full.reshape((n_vis * block.shape[0],) + block.shape[1:]), tied


def reduce_rows(partial, n_vis, rows):
    half = n_vis // 2
    me = lax.axis_index("vis")
    slabs = partial.astype(jnp.bfloat16).reshape((half, 2, rows) + partial.shape[1:])
    groups = [list(range(half)), list(range(half, n_vis))]
    got = lax.all_to_all(slabs, "vis", 0, 0, axis_index_groups=groups)
    acc = jnp.sum(got.astype(jnp.float32), axis=0)
    mine = jnp.where(me < half, acc[0], acc[1])
    send = jnp.where(me < half, acc[1], acc[0]).astype(jnp.bfloat16)
    return mine + exchange(send, n_vis, half).astype(jnp.float32)


def local(
    patch_intensity,
    recorded_samples,
    sample_importance,
    block_populations,
    receiver_pairs,
    sample_rotation_phase,
    spectral_scaling,
    receiver_positions,
    patch_layout_position,
):
    rows_dev = patch_intensity.shape[0]
    ch_local = patch_intensity.shape[1]
    facets_here = patch_intensity.shape[2]
    facet = patch_intensity.shape[3]
    nvis = sample_importance.shape[0]
    n_vis = lax.axis_size("vis")
    image = GRID * facet
    norm_pred = 1.0 / math.sqrt(facets_here * facet * facet)
    norm_grad = 1.0 / math.sqrt(nvis * n_vis)
    sky_half = lax.optimization_barrier(patch_intensity.astype(jnp.bfloat16))
    piece, (receiver_pairs, sample_rotation_phase) = gather_rows(
        sky_half, n_vis, (receiver_pairs, sample_rotation_phase)
    )
    eastward_shift = receiver_lookup_dict(
        receiver_positions[0], receiver_pairs[:, 0]
    ) - receiver_lookup_dict(receiver_positions[0], receiver_pairs[:, 1])
    northward_shift = receiver_lookup_dict(
        receiver_positions[1], receiver_pairs[:, 0]
    ) - receiver_lookup_dict(receiver_positions[1], receiver_pairs[:, 1])
    base_u = eastward_shift * jnp.cos(sample_rotation_phase) - northward_shift * jnp.sin(
        sample_rotation_phase
    )
    base_v = eastward_shift * jnp.sin(sample_rotation_phase) + northward_shift * jnp.cos(
        sample_rotation_phase
    )
    slots = jnp.arange(nvis, dtype=jnp.int32)
    block_count = jnp.broadcast_to(
        block_populations[:, None], (block_populations.shape[0], BLOCK)
    ).reshape(nvis)
    scale_vis = (slots % BLOCK < block_count).astype(jnp.float32) * sample_importance
    first_row = patch_layout_position[:, 0] * facet - image // 2
    first_col = patch_layout_position[:, 1] * facet - image // 2
    chunk = np.arange(n_vis, dtype=np.int32)
    owner = (chunk % 2) * (n_vis // 2) + chunk // 2
    row_starts = first_row[:, None] + jnp.asarray(rows_dev * owner, jnp.int32)[None, :]
    col_offsets = LANE_BLOCK * np.arange(facet // LANE_BLOCK, dtype=np.int32)
    col_starts = first_col[:, None] + jnp.asarray(col_offsets, jnp.int32)[None, :]


    new_rows = []
    residuals = []
    for c in range(ch_local):
        coord_u = spectral_scaling[c] * base_u
        coord_v = spectral_scaling[c] * base_v
        row_factors = phase_factors(coord_u, row_starts, rows_dev, image)
        col_cos, col_sin = phase_table(phase_factors(coord_v, col_starts, LANE_BLOCK, image))
        cols = jnp.concatenate([col_cos, col_sin], axis=2).astype(jnp.bfloat16)
        sky_rows = jnp.transpose(piece[:, c], (1, 0, 2))
        waves = jnp.einsum("fij,fjk->fik", sky_rows, cols, preferred_element_type=jnp.float32)
        wave_c = waves[:, :, :nvis]
        wave_s = waves[:, :, nvis:]
        coarse_c, coarse_s, fine_c, fine_s = row_factors
        faces, chunks, _ = coarse_c.shape
        wave_c = wave_c.reshape(faces, chunks, rows_dev, nvis)
        wave_s = wave_s.reshape(faces, chunks, rows_dev, nvis)
        part_a = jnp.sum(fine_c * wave_c - fine_s * wave_s, axis=2)
        part_b = jnp.sum(fine_s * wave_c + fine_c * wave_s, axis=2)
        sum_re = jnp.sum(coarse_c * part_a - coarse_s * part_b, axis=(0, 1))
        sum_im = -jnp.sum(coarse_c * part_b + coarse_s * part_a, axis=(0, 1))
        resid_real = scale_vis * (norm_pred * sum_re - recorded_samples[c, 0])
        resid_imag = scale_vis * (norm_pred * sum_im - recorded_samples[c, 1])
        fine_c, fine_s = row_factors[2], row_factors[3]
        coarse_c, coarse_s = row_factors[0], row_factors[1]
        turned = (
            coarse_c * resid_real[None, None, :] - coarse_s * resid_imag[None, None, :],
            coarse_s * resid_real[None, None, :] + coarse_c * resid_imag[None, None, :],
        )
        z_one, z_two = rotate(turned, fine_c, fine_s)
        z_one = z_one.astype(jnp.bfloat16)
        z_two = z_two.astype(jnp.bfloat16)
        zs = jnp.concatenate([z_one, -z_two], axis=2)
        grad = jnp.einsum("fik,fjk->ifj", zs, cols, preferred_element_type=jnp.float32)
        new_rows.append(grad)
        residuals.append(jnp.stack([resid_real, resid_imag], axis=0))
    partial = jnp.stack(new_rows, axis=1)
    gradient = reduce_rows(partial, n_vis, rows_dev)
    padded = extended(sky_half, (("chan", 1),), 1).astype(
        patch_intensity.dtype
    )
    left_side = padded[:, :-2]
    right_side = padded[:, 2:]
    chan_index = lax.axis_index("chan") * ch_local + jnp.arange(ch_local, dtype=jnp.int32)
    total_chan = ch_local * lax.axis_size("chan")
    has_left = (chan_index >= 1).astype(jnp.float32)[None, :, None, None]
    has_right = (chan_index <= total_chan - 2).astype(jnp.float32)[None, :, None, None]
    smooth = has_left * (patch_intensity - left_side) + has_right * (patch_intensity - right_side)
    new_sky = patch_intensity - step_size * (norm_grad * gradient + smooth_weight * smooth)
    residual = jnp.stack(residuals, axis=0)
    return (new_sky, residual)


def solution(mesh):
    return jax.shard_map(
        local,
        mesh=mesh,
        in_specs=(
            P("vis", "chan", None, None),
            P("chan", None, "vis"),
            P("vis"),
            P("vis"),
            P("vis", None),
            P("vis"),
            P("chan"),
            P(),
            P(),
        ),
        out_specs=(P("vis", "chan", None, None), P("chan", None, "vis")),
        check_vma=False,
    )
```

```python
import math

import jax
import jax.numpy as jnp
import numpy as np
from jax import lax
from jax.sharding import PartitionSpec as P

GRID = 64
BLOCK = 256
LANE_BLOCK = 128
COORD_STEPS = 16


full_turn = 6.283185307179586
step_size = 0.5
smooth_weight = 0.5


def extended(cells, sides, width):
    for axis, dim in sides:
        count = lax.axis_size(axis)
        ends = count - 1
        head = lax.slice_in_dim(cells, 0, width, axis=dim)
        tail = lax.slice_in_dim(cells, cells.shape[dim] - width, cells.shape[dim], axis=dim)
        cells = jnp.concatenate(
            [
                lax.ppermute(tail, axis, [(i, (i + 1) % count) for i in range(ends)]),
                cells,
                lax.ppermute(head, axis, [((i + 1) % count, i) for i in range(ends)]),
            ],
            axis=dim,
        )
    return cells


def receiver_lookup_dict(table_row, antenna_ids):
    numbers = jnp.arange(table_row.shape[0], dtype=jnp.int32)
    return jnp.sum(
        jnp.where(antenna_ids[:, None] == numbers[None, :], table_row[None, :], 0.0), axis=1
    )


def turns(coord, pixel, image):
    whole = jnp.round(coord * COORD_STEPS).astype(jnp.int32)
    rest = coord - whole.astype(jnp.float32) / COORD_STEPS
    period = COORD_STEPS * image
    exact = jnp.bitwise_and(whole[None, :] * pixel, period - 1).astype(jnp.float32) / period
    return exact + rest[None, :] * pixel.astype(jnp.float32) / image


def phase_factors(coord, starts, span, image):
    faces, chunks = starts.shape
    coarse = full_turn * turns(coord, starts.reshape(-1, 1), image)
    fine = full_turn * turns(coord, jnp.arange(span, dtype=jnp.int32)[:, None], image)
    coarse_c, coarse_s, fine_c, fine_s = lax.optimization_barrier(
        (jnp.cos(coarse), jnp.sin(coarse), jnp.cos(fine), jnp.sin(fine))
    )
    count = coord.shape[0]
    return (
        coarse_c.reshape(faces, chunks, count),
        coarse_s.reshape(faces, chunks, count),
        fine_c,
        fine_s,
    )


def spread(a, span):
    faces, chunks, count = a.shape
    return jnp.broadcast_to(a[:, :, None, :], (faces, chunks, span, count)).reshape(
        faces, chunks * span, count
    )


def tile(a, faces, chunks):
    span, count = a.shape
    return jnp.broadcast_to(a[None, None], (faces, chunks, span, count)).reshape(
        faces, chunks * span, count
    )


def rotate(factors, fine_c, fine_s):
    coarse_c, coarse_s = factors[0], factors[1]
    faces, chunks, _ = coarse_c.shape
    span = fine_c.shape[0]
    pc, ps = spread(coarse_c, span), spread(coarse_s, span)
    qc, qs = tile(fine_c, faces, chunks), tile(fine_s, faces, chunks)
    return (pc * qc - ps * qs, ps * qc + pc * qs)


def phase_table(factors):
    return rotate(factors, factors[2], factors[3])


def exchange(x, n_vis, mask):
    return lax.ppermute(x, "vis", [(i, i ^ mask) for i in range(n_vis)])


def gather_rows(block, n_vis, tied):
    half = n_vis // 2
    me = lax.axis_index("vis")
    other = exchange(block, n_vis, half)
    other, tied = lax.optimization_barrier((other, tied))
    wide = (half, 2) + block.shape
    mine = jnp.broadcast_to(block[None, None], wide)
    theirs = jnp.broadcast_to(other[None, None], wide)
    slot = lax.broadcasted_iota(jnp.int32, wide, 1)
    groups = [list(range(half)), list(range(half, n_vis))]
    full = lax.all_to_all(
        jnp.where((slot == 0) == (me < half), mine, theirs), "vis", 0, 0, axis_index_groups=groups
    )
    return full.reshape((n_vis * block.shape[0],) + block.shape[1:]), tied


def reduce_rows(partial, n_vis, rows):
    half = n_vis // 2
    me = lax.axis_index("vis")
    slabs = partial.astype(jnp.bfloat16).reshape((half, 2, rows) + partial.shape[1:])
    groups = [list(range(half)), list(range(half, n_vis))]
    got = lax.all_to_all(slabs, "vis", 0, 0, axis_index_groups=groups)
    acc = jnp.sum(got.astype(jnp.float32), axis=0)
    mine = jnp.where(me < half, acc[0], acc[1])
    send = jnp.where(me < half, acc[1], acc[0]).astype(jnp.bfloat16)
    return mine + exchange(send, n_vis, half).astype(jnp.float32)


def local(
    patch_intensity,
    recorded_samples,
    sample_importance,
    block_populations,
    receiver_pairs,
    sample_rotation_phase,
    spectral_scaling,
    receiver_positions,
    patch_layout_position,
):
    rows_dev = patch_intensity.shape[0]
    ch_local = patch_intensity.shape[1]
    facets_here = patch_intensity.shape[2]
    facet = patch_intensity.shape[3]
    nvis = sample_importance.shape[0]
    n_vis = lax.axis_size("vis")
    image = GRID * facet
    norm_pred = 1.0 / math.sqrt(facets_here * facet * facet)
    norm_grad = 1.0 / math.sqrt(nvis * n_vis)
    sky_half = lax.optimization_barrier(patch_intensity.astype(jnp.bfloat16))
    piece, (receiver_pairs, sample_rotation_phase) = gather_rows(
        sky_half, n_vis, (receiver_pairs, sample_rotation_phase)
    )
    eastward_shift = receiver_lookup_dict(
        receiver_positions[0], receiver_pairs[:, 0]
    ) - receiver_lookup_dict(receiver_positions[0], receiver_pairs[:, 1])
    northward_shift = receiver_lookup_dict(
        receiver_positions[1], receiver_pairs[:, 0]
    ) - receiver_lookup_dict(receiver_positions[1], receiver_pairs[:, 1])
    base_u = eastward_shift * jnp.cos(sample_rotation_phase) - northward_shift * jnp.sin(
        sample_rotation_phase
    )
    base_v = eastward_shift * jnp.sin(sample_rotation_phase) + northward_shift * jnp.cos(
        sample_rotation_phase
    )
    slots = jnp.arange(nvis, dtype=jnp.int32)
    block_count = jnp.broadcast_to(
        block_populations[:, None], (block_populations.shape[0], BLOCK)
    ).reshape(nvis)
    scale_vis = (slots % BLOCK < block_count).astype(jnp.float32) * sample_importance
    first_row = patch_layout_position[:, 0] * facet - image // 2
    first_col = patch_layout_position[:, 1] * facet - image // 2
    chunk = np.arange(n_vis, dtype=np.int32)
    owner = (chunk % 2) * (n_vis // 2) + chunk // 2
    row_starts = first_row[:, None] + jnp.asarray(rows_dev * owner, jnp.int32)[None, :]
    col_offsets = LANE_BLOCK * np.arange(facet // LANE_BLOCK, dtype=np.int32)
    col_starts = first_col[:, None] + jnp.asarray(col_offsets, jnp.int32)[None, :]


    new_rows = []
    residuals = []
    for c in range(ch_local):
        coord_u = spectral_scaling[c] * base_u
        coord_v = spectral_scaling[c] * base_v
        row_factors = phase_factors(coord_u, row_starts, rows_dev, image)
        col_cos, col_sin = phase_table(phase_factors(coord_v, col_starts, LANE_BLOCK, image))
        cols = jnp.concatenate([col_cos, col_sin], axis=2).astype(jnp.bfloat16)
        sky_rows = jnp.transpose(piece[:, c], (1, 0, 2))
        waves = jnp.einsum("fij,fjk->fik", sky_rows, cols, preferred_element_type=jnp.float32)
        wave_c = waves[:, :, :nvis]
        wave_s = waves[:, :, nvis:]
        coarse_c, coarse_s, fine_c, fine_s = row_factors
        faces, chunks, _ = coarse_c.shape
        wave_c = wave_c.reshape(faces, chunks, rows_dev, nvis)
        wave_s = wave_s.reshape(faces, chunks, rows_dev, nvis)
        part_a = jnp.sum(fine_c * wave_c - fine_s * wave_s, axis=2)
        part_b = jnp.sum(fine_s * wave_c + fine_c * wave_s, axis=2)
        sum_re = jnp.sum(coarse_c * part_a - coarse_s * part_b, axis=(0, 1))
        sum_im = -jnp.sum(coarse_c * part_b + coarse_s * part_a, axis=(0, 1))
        resid_real = scale_vis * (norm_pred * sum_re - recorded_samples[c, 0])
        resid_imag = scale_vis * (norm_pred * sum_im - recorded_samples[c, 1])
        fine_c, fine_s = row_factors[2], row_factors[3]
        coarse_c, coarse_s = row_factors[0], row_factors[1]
        turned = (
            coarse_c * resid_real[None, None, :] - coarse_s * resid_imag[None, None, :],
            coarse_s * resid_real[None, None, :] + coarse_c * resid_imag[None, None, :],
        )
        first = (jnp.concatenate([turned[0], -turned[1]], axis=2), jnp.concatenate([turned[1], turned[0]], axis=2))
        fine_cc = jnp.concatenate([fine_c, fine_c], axis=1)
        fine_ss = jnp.concatenate([fine_s, fine_s], axis=1)
        zs = rotate(first, fine_cc, fine_ss)[0].astype(jnp.bfloat16)
        grad = jnp.einsum("fik,fjk->ifj", zs, cols, preferred_element_type=jnp.float32)
        new_rows.append(grad)
        residuals.append(jnp.stack([resid_real, resid_imag], axis=0))
    partial = jnp.stack(new_rows, axis=1)
    gradient = reduce_rows(partial, n_vis, rows_dev)
    padded = extended(sky_half, (("chan", 1),), 1).astype(
        patch_intensity.dtype
    )
    left_side = padded[:, :-2]
    right_side = padded[:, 2:]
    chan_index = lax.axis_index("chan") * ch_local + jnp.arange(ch_local, dtype=jnp.int32)
    total_chan = ch_local * lax.axis_size("chan")
    has_left = (chan_index >= 1).astype(jnp.float32)[None, :, None, None]
    has_right = (chan_index <= total_chan - 2).astype(jnp.float32)[None, :, None, None]
    smooth = has_left * (patch_intensity - left_side) + has_right * (patch_intensity - right_side)
    new_sky = patch_intensity - step_size * (norm_grad * gradient + smooth_weight * smooth)
    residual = jnp.stack(residuals, axis=0)
    return (new_sky, residual)


def solution(mesh):
    return jax.shard_map(
        local,
        mesh=mesh,
        in_specs=(
            P("vis", "chan", None, None),
            P("chan", None, "vis"),
            P("vis"),
            P("vis"),
            P("vis", None),
            P("vis"),
            P("chan"),
            P(),
            P(),
        ),
        out_specs=(P("vis", "chan", None, None), P("chan", None, "vis")),
        check_vma=False,
    )
```
